32 devices in a mesh: groups: 2 (over x), band: 16 (over z, y, core).
Axes of the slice: x: 2, y: 2, z: 4, core: 2. Of those that a mesh axis runs over, the one named last changes fastest.
Arguments:
- initial_height_velocity: float32 [64, 3, 16, 512], P(('groups', 'band')), parts along dimension 0, may hold values from -3 to 3
- member_fidelity: int32 [64], P('groups'), parts along dimension 0, may hold values from 0 to 2, as said below
- obs_cell: int32 [32, 256], P(('groups', 'band')), parts along dimension 0, may hold values from 0 to 4607, as said below
- obs_value: float32 [32, 256], P(('groups', 'band')), parts along dimension 0, may hold values from -3 to 3
- obs_var: float32 [32, 256], P(('groups', 'band')), parts along dimension 0, may hold values from 0.04 to 0.4
- obs_noise: float32 [32, 256, 32], P(('groups', 'band')), parts along dimension 0, may hold values from -6 to 6
Outputs:
- analysis: float32 [64, 3, 16, 512], P(('groups', 'band')), parts along dimension 0
The draws below stay inside these ranges and needn't reach their ends.
There are 2 independent parts, one for each index of `groups`. The reference program is written for one: setup_inputs(seed, part) draws one part's arguments, and reference() takes and returns one part's arrays. A program takes and returns all parts, laid end to end along the dimension named above; each array names one. Nothing has to cross between parts.
Inputs may be any that keep to these rules, and one draw needn't show every extreme that they name: `member_fidelity`: exactly half of the 32 members have class 0, a quarter class 1 and a quarter class 2. `obs_cell`: an entry is c * 3 * 512 + r * 512 + j for component c, row r of the tile's extended block and column j; the row always lies inside the grid. Observation 0 of tile 1 is 0 and observation 1 of tile 1 is the largest value.
All inputs are finite; a program needn't handle non-finite values.
Results may differ from the reference program's by a relative error of at most 0.0003.
Values sent between devices are 32-bit elements; how exact they have to be, the bound alone decides.
No kernel may reach another device: no remote copies, remote signals or barrier semaphores. Data moves between devices by JAX's collectives and lax.ppermute only.
A program may use at most 64 MiB of HBM per device.

```python
import math
import jax
import jax.numpy as jnp
from jax import lax

ROWS_PER_TILE = 1
NLON = 512
OBS = 256
PREDICTION_COUNT = 4
MEMBERS = 32
TILES = 16
NLAT = 16


def draw_member_fidelity(key, part):
    shuffled = jax.random.permutation(key, MEMBERS)
    return ((shuffled >= MEMBERS // 2).astype(jnp.int32) + (shuffled >= 3 * MEMBERS // 4).astype(jnp.int32)).astype(jnp.int32)


def draw_obs_cell(key, part):
    key_field = jax.random.fold_in(key, 11)
    key_row = jax.random.fold_in(key, 12)
    key_col = jax.random.fold_in(key, 13)
    component = jax.random.randint(key_field, (TILES, OBS), 0, 3)
    tile_ids = jnp.arange(TILES)[:, None]
    lowest = jnp.where(tile_ids == 0, ROWS_PER_TILE, 0)
    highest = jnp.where(tile_ids == TILES - 1, 2 * ROWS_PER_TILE, 3 * ROWS_PER_TILE)
    row_pick = jax.random.randint(key_row, (TILES, OBS), lowest, highest)
    column = jax.random.randint(key_col, (TILES, OBS), 0, NLON)
    places = component * (3 * ROWS_PER_TILE * NLON) + row_pick * NLON + column
    places = places.at[1, 0].set(0).at[1, 1].set(9 * ROWS_PER_TILE * NLON - 1)
    return places.astype(jnp.int32)


def steps_of(stream_key, extent, split, least, top_value):
    gain, own = 1.0, jax.random.fold_in(stream_key, 6)
    for axis_at, blocks in split:
        steps = jnp.exp(jax.random.uniform(jax.random.fold_in(own, axis_at), (blocks,), jnp.float32, least / len(split), top_value / len(split)))
        gain = gain * jnp.repeat(steps, extent[axis_at] // blocks).reshape([-1 if axis == axis_at else 1 for axis in range(len(extent))])
    return gain


def bell_draw(own_key, shape, scale, most, cuts=(), dtype=jnp.bfloat16):
    entries = scale * jax.random.normal(own_key, shape, jnp.float32)
    if cuts:
        entries = entries * steps_of(own_key, shape, cuts, -0.22, 0.18)
    return jnp.clip(entries, -most, most).astype(dtype)


def setup_inputs(seed: int = 0, part: int = 0) -> dict:
    arg_keys = jax.random.split(jax.random.key(seed), 7)
    part_keys = jax.random.split(jax.random.fold_in(arg_keys[6], part), 7)
    return {
        "initial_height_velocity": bell_draw(part_keys[0], (MEMBERS, 3, NLAT, NLON), 0.2, 3.0, ((0, 16),), jnp.float32),
        "member_fidelity": draw_member_fidelity(jax.random.fold_in(jax.random.fold_in(arg_keys[6], part), 71), part),
        "obs_cell": draw_obs_cell(jax.random.fold_in(jax.random.fold_in(arg_keys[6], part), 71), part),
        "obs_value": bell_draw(part_keys[3], (TILES, OBS), 0.2, 3.0, ((0, 16),), jnp.float32),
        "obs_var": jnp.clip(jnp.exp(math.log(0.4) - 2.3025851 * jax.random.uniform(part_keys[4], (TILES, OBS), jnp.float32) ** steps_of(part_keys[4], (TILES, OBS), ((0, 16),), -0.2, 0.2)), 0.04, 0.4),
        "obs_noise": bell_draw(part_keys[5], (TILES, OBS, MEMBERS), 1.0, 6.0, ((0, 16),), jnp.float32),
    }


exact = lax.Precision.HIGHEST
time_step = 0.25
viscous = 0.05
slow_friction = 0.2
control_weight = 0.5

def neighbours(field):
    lon_pad = jnp.pad(field, [(0, 0)] * (field.ndim - 1) + [(1, 1)])
    lat_pad = jnp.pad(field, [(0, 0)] * (field.ndim - 2) + [(1, 1), (0, 0)])
    return (lon_pad[..., 2:], lon_pad[..., :-2], lat_pad[..., 2:, :], lat_pad[..., :-2, :])

def east_slope(field):
    ahead, behind, upper, lower = neighbours(field)
    return 0.5 * (ahead - behind)

def north_slope(field):
    ahead, behind, upper, lower = neighbours(field)
    return 0.5 * (upper - lower)

def laplace(field):
    ahead, behind, upper, lower = neighbours(field)
    return ahead + behind + upper + lower - 4.0 * field

def advance(height, eastward, northward, nonlinear, friction, coriolis):
    depth = 1.0 + nonlinear * height
    height_new = height - time_step * (east_slope(depth * eastward) + north_slope(depth * northward)) + time_step * viscous * laplace(height)
    east_new = eastward + time_step * (-nonlinear * (eastward * east_slope(eastward) + northward * north_slope(eastward)) + coriolis * northward - east_slope(height_new) + viscous * laplace(eastward) - friction * eastward)
    north_new = northward + time_step * (-nonlinear * (eastward * east_slope(northward) + northward * north_slope(northward)) - coriolis * eastward - north_slope(height_new) + viscous * laplace(northward) - friction * northward)
    return (height_new, east_new, north_new)

def begin_prediction(marine_condition, accuracy_levels, realization_count):
    nonlinear = (accuracy_levels == 0).astype(jnp.float32)[:, None, None]
    friction = jnp.where(accuracy_levels == 0, 0.0, slow_friction).astype(jnp.float32)[:, None, None]
    lat_rows = marine_condition.shape[2]
    coriolis = (0.1 + 0.2 * (jnp.arange(lat_rows).astype(jnp.float32) + 0.5) / lat_rows)[:, None]
    height, eastward, northward = (marine_condition[:, 0], marine_condition[:, 1], marine_condition[:, 2])
    for step in range(realization_count):
        height, eastward, northward = advance(height, eastward, northward, nonlinear, friction, coriolis)
    return jnp.stack([height, eastward, northward], axis=1)

def class_tables(accuracy_levels):
    onehot = (accuracy_levels[:, None] == jnp.arange(3)[None, :]).astype(jnp.float32)
    counts = lax.optimization_barrier(jnp.sum(onehot, axis=0))
    coefs = jnp.stack([1.0 / (counts[0] - 1.0), -control_weight / (counts[1] - 1.0), control_weight / (counts[2] - 1.0)])
    member_weight = lax.optimization_barrier(jnp.sum(onehot * coefs[None, :], axis=1))
    return (onehot, counts, member_weight)

def remove_means(data, onehot, counts):
    means = jnp.dot(onehot.T, data, precision=exact) / counts[:, None]
    return data - jnp.dot(onehot, means, precision=exact)

def spd_solve(factor, rhs):
    inner = lax.linalg.triangular_solve(factor, rhs, left_side=True, lower=True)
    return lax.linalg.triangular_solve(factor, inner, left_side=True, lower=True, transpose_a=True)

def analyse(tile_worker, observed, accuracy_levels, values, variance, noise):
    ensemble_members = tile_worker.shape[0]
    onehot, counts, member_weight = class_tables(accuracy_levels)
    flat = tile_worker.reshape(ensemble_members, -1)
    spread = remove_means(flat, onehot, counts)
    obs_spread = remove_means(observed, onehot, counts)
    principal = onehot[:, 0] / (counts[0] - 1.0)
    innovation_cov = jnp.dot((obs_spread * principal[:, None]).T, obs_spread, precision=exact) + jnp.diag(variance)
    perturbed = values[:, None] + jnp.sqrt(variance)[:, None] * noise - observed.T
    factor = jnp.linalg.cholesky(innovation_cov)
    solved = spd_solve(factor, perturbed)
    mixing = jnp.dot(obs_spread, solved, precision=exact) * member_weight[:, None]
    update = jnp.dot(mixing.T, spread, precision=exact)
    return (flat + update).reshape(tile_worker.shape)

def reference(initial_height_velocity, member_fidelity, obs_cell, obs_value, obs_var, obs_noise):

    def advance_single(class_member_pair):
        lone_condition, accuracy_level_one = class_member_pair
        return begin_prediction(lone_condition[None], accuracy_level_one[None], PREDICTION_COUNT)[0]
    integrate_realizations = lax.map(advance_single, (initial_height_velocity, member_fidelity))
    ensemble_members = integrate_realizations.shape[0]
    halo_padded = jnp.pad(integrate_realizations, ((0, 0), (0, 0), (ROWS_PER_TILE, ROWS_PER_TILE), (0, 0)))

    def one_tile(tile_index):
        start = (tile_index * ROWS_PER_TILE).astype(jnp.int32)
        block = lax.dynamic_slice_in_dim(halo_padded, start, 3 * ROWS_PER_TILE, 2)
        tile_worker = block[:, :, ROWS_PER_TILE:2 * ROWS_PER_TILE]
        observed = jnp.take(block.reshape(ensemble_members, -1), obs_cell[tile_index], axis=1)
        return analyse(tile_worker, observed, member_fidelity, obs_value[tile_index], obs_var[tile_index], obs_noise[tile_index])
    tiles = lax.map(one_tile, jnp.arange(TILES).astype(jnp.int32))
    return jnp.moveaxis(tiles, 0, 2).reshape(ensemble_members, 3, TILES * ROWS_PER_TILE, NLON)
```

```python
import jax
import jax.numpy as jnp
from jax import lax
from jax.sharding import PartitionSpec as P
from jax.experimental import pallas as pl
from jax.experimental.pallas import tpu as pltpu

PREDICTION_COUNT = 4


exact = lax.Precision.HIGHEST
time_step = 0.25
viscous = 0.05
slow_friction = 0.2
control_weight = 0.5


def extended(shard, sides, width):
    for axis, dim in sides:
        devices, length = (lax.axis_size(axis), shard.shape[dim])
        up = [(i, (i + 1) % devices) for i in range(devices - 1)]
        down = [(j, i) for i, j in up]
        last = lax.slice_in_dim(shard, length - width, length, axis=dim)
        leading = lax.slice_in_dim(shard, 0, width, axis=dim)
        before = lax.ppermute(last, axis, up)
        after = lax.ppermute(leading, axis, down)
        shard = jnp.concatenate([before, shard, after], axis=dim)
    return shard


def neighbours(field):
    lon_pad = jnp.pad(field, [(0, 0)] * (field.ndim - 1) + [(1, 1)])
    lat_pad = jnp.pad(field, [(0, 0)] * (field.ndim - 2) + [(1, 1), (0, 0)])
    return (lon_pad[..., 2:], lon_pad[..., :-2], lat_pad[..., 2:, :], lat_pad[..., :-2, :])


def east_slope(field):
    ahead, behind, upper, lower = neighbours(field)
    return 0.5 * (ahead - behind)


def north_slope(field):
    ahead, behind, upper, lower = neighbours(field)
    return 0.5 * (upper - lower)


def laplace(field):
    ahead, behind, upper, lower = neighbours(field)
    return ahead + behind + upper + lower - 4.0 * field


def advance(height, eastward, northward, nonlinear, friction, coriolis):
    depth = 1.0 + nonlinear * height
    height_new = (
        height
        - time_step * (east_slope(depth * eastward) + north_slope(depth * northward))
        + time_step * viscous * laplace(height)
    )
    east_new = eastward + time_step * (
        -nonlinear * (eastward * east_slope(eastward) + northward * north_slope(eastward))
        + coriolis * northward
        - east_slope(height_new)
        + viscous * laplace(eastward)
        - friction * eastward
    )
    north_new = northward + time_step * (
        -nonlinear * (eastward * east_slope(northward) + northward * north_slope(northward))
        - coriolis * eastward
        - north_slope(height_new)
        + viscous * laplace(northward)
        - friction * northward
    )
    return (height_new, east_new, north_new)


def begin_prediction(marine_condition, accuracy_levels, realization_count):
    nonlinear = (accuracy_levels == 0).astype(jnp.float32)[:, None, None]
    friction = jnp.where(accuracy_levels == 0, 0.0, slow_friction).astype(jnp.float32)[
        :, None, None
    ]
    lat_rows = marine_condition.shape[2]
    coriolis = (0.1 + 0.2 * (jnp.arange(lat_rows).astype(jnp.float32) + 0.5) / lat_rows)[:, None]
    height, eastward, northward = (
        marine_condition[:, 0],
        marine_condition[:, 1],
        marine_condition[:, 2],
    )
    for step in range(realization_count):
        height, eastward, northward = advance(
            height, eastward, northward, nonlinear, friction, coriolis
        )
    return jnp.stack([height, eastward, northward], axis=1)


def class_tables(accuracy_levels):
    onehot = (accuracy_levels[:, None] == jnp.arange(3)[None, :]).astype(jnp.float32)
    counts = jnp.sum(onehot, axis=0)
    coefs = jnp.stack(
        [
            1.0 / (counts[0] - 1.0),
            -control_weight / (counts[1] - 1.0),
            control_weight / (counts[2] - 1.0),
        ]
    )
    member_weight = jnp.sum(onehot * coefs[None, :], axis=1)
    return (onehot, counts, member_weight)


def remove_means(data, onehot, counts):
    means = jnp.dot(onehot.T, data, precision=exact) / counts[:, None]
    return data - jnp.dot(onehot, means, precision=exact)


def spd_solve(factor, rhs):
    inner = lax.linalg.triangular_solve(factor, rhs, left_side=True, lower=True)
    return lax.linalg.triangular_solve(factor, inner, left_side=True, lower=True, transpose_a=True)


def gauss_jordan_kernel(a_ref, o_ref):
    n = a_ref.shape[0]
    lane = lax.broadcasted_iota(jnp.int32, a_ref.shape, 1)
    row_id = lax.broadcasted_iota(jnp.int32, (n, 1), 0)

    def step(k, a):
        pivot_row = jnp.sum(jnp.where(row_id == k, a, 0.0), axis=0, keepdims=True)
        column = jnp.sum(jnp.where(lane == k, a, 0.0), axis=1, keepdims=True)
        pivot = jnp.sum(jnp.where(lane[0:1] == k, pivot_row, 0.0), axis=1, keepdims=True)
        pivot_row = pivot_row / pivot
        column = column - (row_id == k).astype(jnp.float32)
        return a - column * pivot_row

    a = lax.fori_loop(0, n, step, a_ref[...], unroll=n <= 64)
    o_ref[...] = a[:, n:]


def gauss_jordan(augmented):
    n = augmented.shape[0]
    return pl.pallas_call(
        gauss_jordan_kernel,
        out_shape=jax.ShapeDtypeStruct((n, augmented.shape[1] - n), jnp.float32),
        in_specs=[pl.BlockSpec(memory_space=pltpu.VMEM)],
        out_specs=pl.BlockSpec(memory_space=pltpu.VMEM),
    )(augmented)


def shards(initial_height_velocity, member_fidelity, obs_cell, obs_value, obs_var, obs_noise):
    per_device = initial_height_velocity.shape[0]
    resident_realizations = lax.dynamic_slice_in_dim(
        member_fidelity, lax.axis_index("band") * per_device, per_device
    )
    integrate_realizations = begin_prediction(
        initial_height_velocity, resident_realizations, PREDICTION_COUNT
    )
    tile_worker = lax.all_to_all(
        integrate_realizations, "band", split_axis=2, concat_axis=0, tiled=True
    )
    ensemble_members = tile_worker.shape[0]
    tile_rows = tile_worker.shape[2]
    flat = tile_worker.reshape(ensemble_members, -1)
    block = extended(tile_worker, (("band", 2),), tile_rows)
    observed = jnp.take(block.reshape(ensemble_members, -1), obs_cell[0], axis=1)
    onehot, counts, member_weight = class_tables(member_fidelity)
    spread = remove_means(flat, onehot, counts)
    obs_spread = remove_means(observed, onehot, counts)
    variance = obs_var[0]
    principal = onehot[:, 0] / (counts[0] - 1.0)
    scale = jnp.sqrt(principal)
    perturbed = obs_value[0][:, None] + jnp.sqrt(variance)[:, None] * obs_noise[0] - observed.T
    weighted = obs_spread / variance[None, :]
    both = jnp.dot(
        weighted, jnp.concatenate([obs_spread.T, perturbed], axis=1), precision=exact
    )
    inner, direct = both[:, :ensemble_members], both[:, ensemble_members:]
    system = jnp.eye(ensemble_members, dtype=jnp.float32) + scale[:, None] * inner * scale[None, :]
    solved = gauss_jordan(jnp.concatenate([system, scale[:, None] * direct], axis=1))
    projected = direct - jnp.dot(inner, scale[:, None] * solved, precision=exact)
    mixing = projected * member_weight[:, None]
    update = jnp.dot(mixing.T, spread, precision=exact)
    result = (flat + update).reshape(tile_worker.shape)
    return lax.all_to_all(result, "band", split_axis=0, concat_axis=2, tiled=True)


def solution(mesh):
    in_specs = (
        P(("groups", "band"), None, None, None),
        P("groups"),
        P(("groups", "band"), None),
        P(("groups", "band"), None),
        P(("groups", "band"), None),
        P(("groups", "band"), None, None),
    )
    out_specs = P(("groups", "band"), None, None, None)
    return jax.shard_map(shards, mesh=mesh, in_specs=in_specs, out_specs=out_specs, check_vma=False)
```

```python
import jax
import jax.numpy as jnp
from jax import lax
from jax.sharding import PartitionSpec as P
from jax.experimental import pallas as pl
from jax.experimental.pallas import tpu as pltpu

PREDICTION_COUNT = 4


exact = lax.Precision.HIGHEST
time_step = 0.25
viscous = 0.05
slow_friction = 0.2
control_weight = 0.5


def extended(shard, sides, width):
    for axis, dim in sides:
        devices, length = (lax.axis_size(axis), shard.shape[dim])
        up = [(i, (i + 1) % devices) for i in range(devices - 1)]
        down = [(j, i) for i, j in up]
        last = lax.slice_in_dim(shard, length - width, length, axis=dim)
        leading = lax.slice_in_dim(shard, 0, width, axis=dim)
        before = lax.ppermute(last, axis, up)
        after = lax.ppermute(leading, axis, down)
        shard = jnp.concatenate([before, shard, after], axis=dim)
    return shard


def neighbours(field):
    lon_pad = jnp.pad(field, [(0, 0)] * (field.ndim - 1) + [(1, 1)])
    lat_pad = jnp.pad(field, [(0, 0)] * (field.ndim - 2) + [(1, 1), (0, 0)])
    return (lon_pad[..., 2:], lon_pad[..., :-2], lat_pad[..., 2:, :], lat_pad[..., :-2, :])


def east_slope(field):
    ahead, behind, upper, lower = neighbours(field)
    return 0.5 * (ahead - behind)


def north_slope(field):
    ahead, behind, upper, lower = neighbours(field)
    return 0.5 * (upper - lower)


def laplace(field):
    ahead, behind, upper, lower = neighbours(field)
    return ahead + behind + upper + lower - 4.0 * field


def advance(height, eastward, northward, nonlinear, friction, coriolis):
    depth = 1.0 + nonlinear * height
    height_new = (
        height
        - time_step * (east_slope(depth * eastward) + north_slope(depth * northward))
        + time_step * viscous * laplace(height)
    )
    east_new = eastward + time_step * (
        -nonlinear * (eastward * east_slope(eastward) + northward * north_slope(eastward))
        + coriolis * northward
        - east_slope(height_new)
        + viscous * laplace(eastward)
        - friction * eastward
    )
    north_new = northward + time_step * (
        -nonlinear * (eastward * east_slope(northward) + northward * north_slope(northward))
        - coriolis * eastward
        - north_slope(height_new)
        + viscous * laplace(northward)
        - friction * northward
    )
    return (height_new, east_new, north_new)


def begin_prediction(marine_condition, accuracy_levels, realization_count):
    nonlinear = (accuracy_levels == 0).astype(jnp.float32)[:, None, None]
    friction = jnp.where(accuracy_levels == 0, 0.0, slow_friction).astype(jnp.float32)[
        :, None, None
    ]
    lat_rows = marine_condition.shape[2]
    coriolis = (0.1 + 0.2 * (jnp.arange(lat_rows).astype(jnp.float32) + 0.5) / lat_rows)[:, None]
    height, eastward, northward = (
        marine_condition[:, 0],
        marine_condition[:, 1],
        marine_condition[:, 2],
    )
    for step in range(realization_count):
        height, eastward, northward = advance(
            height, eastward, northward, nonlinear, friction, coriolis
        )
    return jnp.stack([height, eastward, northward], axis=1)


def class_tables(accuracy_levels):
    onehot = (accuracy_levels[:, None] == jnp.arange(3)[None, :]).astype(jnp.float32)
    counts = jnp.sum(onehot, axis=0)
    coefs = jnp.stack(
        [
            1.0 / (counts[0] - 1.0),
            -control_weight / (counts[1] - 1.0),
            control_weight / (counts[2] - 1.0),
        ]
    )
    member_weight = jnp.sum(onehot * coefs[None, :], axis=1)
    return (onehot, counts, member_weight)


def remove_means(data, onehot, counts):
    means = jnp.dot(onehot.T, data, precision=exact) / counts[:, None]
    return data - jnp.dot(onehot, means, precision=exact)


def spd_solve(factor, rhs):
    inner = lax.linalg.triangular_solve(factor, rhs, left_side=True, lower=True)
    return lax.linalg.triangular_solve(factor, inner, left_side=True, lower=True, transpose_a=True)


def gauss_jordan_steps(a):
    n = a.shape[0]
    lane = lax.broadcasted_iota(jnp.int32, a.shape, 1)
    row_id = lax.broadcasted_iota(jnp.int32, (n, 1), 0)

    def step(k, a):
        pivot_row = jnp.sum(jnp.where(row_id == k, a, 0.0), axis=0, keepdims=True)
        column = jnp.sum(jnp.where(lane == k, a, 0.0), axis=1, keepdims=True)
        pivot = jnp.sum(jnp.where(lane[0:1] == k, pivot_row, 0.0), axis=1, keepdims=True)
        pivot_row = pivot_row / pivot
        column = column - (row_id == k).astype(jnp.float32)
        return a - column * pivot_row

    return lax.fori_loop(0, n, step, a, unroll=n <= 64)

def contract(a, b, dims):
    return lax.dot_general(
        a, b, (dims, ((), ())), precision=exact, preferred_element_type=jnp.float32
    )


def analysis_kernel(x_ref, ob_ref, fid_col_ref, fid_row_ref, value_ref, var_ref, noise_ref, o_ref):
    m = x_ref.shape[0]
    x = x_ref[...]
    ob = ob_ref[...]
    fid_col = fid_col_ref[...]
    fid_row = fid_row_ref[...]
    variance = var_ref[...]
    masks = [(fid_col == c).astype(jnp.float32) for c in range(3)]
    masks_row = [(fid_row == c).astype(jnp.float32) for c in range(3)]
    counts = [jnp.sum(mask, axis=0, keepdims=True) for mask in masks]

    def remove_means(data):
        centred = data
        for mask, count in zip(masks, counts):
            centred = centred - mask * (jnp.sum(mask * data, axis=0, keepdims=True) / count)
        return centred

    spread = remove_means(x)
    obs_spread = remove_means(ob)
    weight = (
        masks[0] * (1.0 / (counts[0] - 1.0))
        + masks[1] * (-control_weight / (counts[1] - 1.0))
        + masks[2] * (control_weight / (counts[2] - 1.0))
    )
    scale_col = jnp.sqrt(masks[0] / (counts[0] - 1.0))
    count_row = jnp.sum(masks_row[0], axis=1, keepdims=True)
    scale_row = jnp.sqrt(masks_row[0] / (count_row - 1.0))
    weighted = obs_spread / variance
    inner = contract(weighted, obs_spread, ((1,), (1,)))
    direct = (
        jnp.sum(weighted * value_ref[...], axis=1, keepdims=True)
        + contract(weighted * jnp.sqrt(variance), noise_ref[...], ((1,), (0,)))
        - contract(weighted, ob, ((1,), (1,)))
    )
    row_id = lax.broadcasted_iota(jnp.int32, (m, m), 0)
    col_id = lax.broadcasted_iota(jnp.int32, (m, m), 1)
    system = (row_id == col_id).astype(jnp.float32) + scale_col * inner * scale_row
    augmented = jnp.concatenate([system, scale_col * direct], axis=1)
    solved = gauss_jordan_steps(augmented)[:, m:]
    projected = direct - contract(inner, scale_col * solved, ((1,), (0,)))
    mixing = projected * weight
    o_ref[...] = x + contract(mixing, spread, ((0,), (0,)))


def analysis(flat, observed, fidelity, value, variance, noise):
    m = flat.shape[0]
    vmem = pl.BlockSpec(memory_space=pltpu.VMEM)
    return pl.pallas_call(
        analysis_kernel,
        out_shape=jax.ShapeDtypeStruct(flat.shape, jnp.float32),
        in_specs=[vmem] * 7,
        out_specs=vmem,
        compiler_params=pltpu.CompilerParams(vmem_limit_bytes=48 * 1024 * 1024),
    )(
        flat,
        observed,
        fidelity.reshape(m, 1),
        fidelity.reshape(1, m),
        value.reshape(1, -1),
        variance.reshape(1, -1),
        noise,
    )


def shards(initial_height_velocity, member_fidelity, obs_cell, obs_value, obs_var, obs_noise):
    per_device = initial_height_velocity.shape[0]
    resident_realizations = lax.dynamic_slice_in_dim(
        member_fidelity, lax.axis_index("band") * per_device, per_device
    )
    integrate_realizations = begin_prediction(
        initial_height_velocity, resident_realizations, PREDICTION_COUNT
    )
    tile_worker = lax.all_to_all(
        integrate_realizations, "band", split_axis=2, concat_axis=0, tiled=True
    )
    ensemble_members = tile_worker.shape[0]
    tile_rows = tile_worker.shape[2]
    flat = tile_worker.reshape(ensemble_members, -1)
    block = extended(tile_worker, (("band", 2),), tile_rows)
    observed = jnp.take(block.reshape(ensemble_members, -1), obs_cell[0], axis=1)
    result = analysis(
        flat,
        observed,
        member_fidelity,
        obs_value[0],
        obs_var[0],
        obs_noise[0],
    ).reshape(tile_worker.shape)
    return lax.all_to_all(result, "band", split_axis=0, concat_axis=2, tiled=True)


def solution(mesh):
    in_specs = (
        P(("groups", "band"), None, None, None),
        P("groups"),
        P(("groups", "band"), None),
        P(("groups", "band"), None),
        P(("groups", "band"), None),
        P(("groups", "band"), None, None),
    )
    out_specs = P(("groups", "band"), None, None, None)
    return jax.shard_map(shards, mesh=mesh, in_specs=in_specs, out_specs=out_specs, check_vma=False)
```

```python
import jax
import jax.numpy as jnp
from jax import lax
from jax.sharding import PartitionSpec as P
from jax.experimental import pallas as pl
from jax.experimental.pallas import tpu as pltpu

PREDICTION_COUNT = 4


exact = lax.Precision.HIGHEST
time_step = 0.25
viscous = 0.05
slow_friction = 0.2
control_weight = 0.5


def extended(shard, sides, width):
    for axis, dim in sides:
        devices, length = (lax.axis_size(axis), shard.shape[dim])
        up = [(i, (i + 1) % devices) for i in range(devices - 1)]
        down = [(j, i) for i, j in up]
        last = lax.slice_in_dim(shard, length - width, length, axis=dim)
        leading = lax.slice_in_dim(shard, 0, width, axis=dim)
        before = lax.ppermute(last, axis, up)
        after = lax.ppermute(leading, axis, down)
        shard = jnp.concatenate([before, shard, after], axis=dim)
    return shard


def neighbours(field):
    lon_pad = jnp.pad(field, [(0, 0)] * (field.ndim - 1) + [(1, 1)])
    lat_pad = jnp.pad(field, [(0, 0)] * (field.ndim - 2) + [(1, 1), (0, 0)])
    return (lon_pad[..., 2:], lon_pad[..., :-2], lat_pad[..., 2:, :], lat_pad[..., :-2, :])


def east_slope(field):
    ahead, behind, upper, lower = neighbours(field)
    return 0.5 * (ahead - behind)


def north_slope(field):
    ahead, behind, upper, lower = neighbours(field)
    return 0.5 * (upper - lower)


def laplace(field):
    ahead, behind, upper, lower = neighbours(field)
    return ahead + behind + upper + lower - 4.0 * field


def advance(height, eastward, northward, nonlinear, friction, coriolis):
    depth = 1.0 + nonlinear * height
    height_new = (
        height
        - time_step * (east_slope(depth * eastward) + north_slope(depth * northward))
        + time_step * viscous * laplace(height)
    )
    east_new = eastward + time_step * (
        -nonlinear * (eastward * east_slope(eastward) + northward * north_slope(eastward))
        + coriolis * northward
        - east_slope(height_new)
        + viscous * laplace(eastward)
        - friction * eastward
    )
    north_new = northward + time_step * (
        -nonlinear * (eastward * east_slope(northward) + northward * north_slope(northward))
        - coriolis * eastward
        - north_slope(height_new)
        + viscous * laplace(northward)
        - friction * northward
    )
    return (height_new, east_new, north_new)


def begin_prediction(marine_condition, accuracy_levels, realization_count):
    nonlinear = (accuracy_levels == 0).astype(jnp.float32)[:, None, None]
    friction = jnp.where(accuracy_levels == 0, 0.0, slow_friction).astype(jnp.float32)[
        :, None, None
    ]
    lat_rows = marine_condition.shape[2]
    coriolis = (0.1 + 0.2 * (jnp.arange(lat_rows).astype(jnp.float32) + 0.5) / lat_rows)[:, None]
    height, eastward, northward = (
        marine_condition[:, 0],
        marine_condition[:, 1],
        marine_condition[:, 2],
    )
    for step in range(realization_count):
        height, eastward, northward = advance(
            height, eastward, northward, nonlinear, friction, coriolis
        )
    return jnp.stack([height, eastward, northward], axis=1)


def class_tables(accuracy_levels):
    onehot = (accuracy_levels[:, None] == jnp.arange(3)[None, :]).astype(jnp.float32)
    counts = jnp.sum(onehot, axis=0)
    coefs = jnp.stack(
        [
            1.0 / (counts[0] - 1.0),
            -control_weight / (counts[1] - 1.0),
            control_weight / (counts[2] - 1.0),
        ]
    )
    member_weight = jnp.sum(onehot * coefs[None, :], axis=1)
    return (onehot, counts, member_weight)


def remove_means(data, onehot, counts):
    means = jnp.dot(onehot.T, data, precision=exact) / counts[:, None]
    return data - jnp.dot(onehot, means, precision=exact)


def spd_solve(factor, rhs):
    inner = lax.linalg.triangular_solve(factor, rhs, left_side=True, lower=True)
    return lax.linalg.triangular_solve(factor, inner, left_side=True, lower=True, transpose_a=True)


def gauss_jordan_steps(a):
    n = a.shape[0]
    lane = lax.broadcasted_iota(jnp.int32, a.shape, 1)
    row_id = lax.broadcasted_iota(jnp.int32, (n, 1), 0)
    if n <= 64:
        for k in range(n):
            pivot_row = a[k : k + 1, :] * (1.0 / a[k : k + 1, k : k + 1])
            column = a[:, k : k + 1] - (row_id == k).astype(jnp.float32)
            a = a - column * pivot_row
        return a

    def step(k, a):
        pivot_row = jnp.sum(jnp.where(row_id == k, a, 0.0), axis=0, keepdims=True)
        column = jnp.sum(jnp.where(lane == k, a, 0.0), axis=1, keepdims=True)
        pivot = jnp.sum(jnp.where(lane[0:1] == k, pivot_row, 0.0), axis=1, keepdims=True)
        pivot_row = pivot_row / pivot
        column = column - (row_id == k).astype(jnp.float32)
        return a - column * pivot_row

    return lax.fori_loop(0, n, step, a)

def contract(a, b, dims):
    return lax.dot_general(
        a, b, (dims, ((), ())), precision=exact, preferred_element_type=jnp.float32
    )


def analysis_kernel(x_ref, ob_ref, fid_col_ref, fid_row_ref, value_ref, var_ref, noise_ref, o_ref):
    m = x_ref.shape[0]
    x = x_ref[...]
    ob = ob_ref[...]
    fid_col = fid_col_ref[...]
    fid_row = fid_row_ref[...]
    variance = var_ref[...]
    masks = [(fid_col == c).astype(jnp.float32) for c in range(3)]
    masks_row = [(fid_row == c).astype(jnp.float32) for c in range(3)]
    counts = [jnp.sum(mask, axis=0, keepdims=True) for mask in masks]

    def remove_means(data):
        centred = data
        for mask, count in zip(masks, counts):
            centred = centred - mask * (jnp.sum(mask * data, axis=0, keepdims=True) / count)
        return centred

    spread = remove_means(x)
    obs_spread = remove_means(ob)
    weight = (
        masks[0] * (1.0 / (counts[0] - 1.0))
        + masks[1] * (-control_weight / (counts[1] - 1.0))
        + masks[2] * (control_weight / (counts[2] - 1.0))
    )
    scale_col = jnp.sqrt(masks[0] / (counts[0] - 1.0))
    count_row = jnp.sum(masks_row[0], axis=1, keepdims=True)
    scale_row = jnp.sqrt(masks_row[0] / (count_row - 1.0))
    weighted = obs_spread / variance
    inner = contract(weighted, obs_spread, ((1,), (1,)))
    direct = (
        jnp.sum(weighted * value_ref[...], axis=1, keepdims=True)
        + contract(weighted * jnp.sqrt(variance), noise_ref[...], ((1,), (0,)))
        - contract(weighted, ob, ((1,), (1,)))
    )
    row_id = lax.broadcasted_iota(jnp.int32, (m, m), 0)
    col_id = lax.broadcasted_iota(jnp.int32, (m, m), 1)
    system = (row_id == col_id).astype(jnp.float32) + scale_col * inner * scale_row
    augmented = jnp.concatenate([system, scale_col * direct], axis=1)
    solved = gauss_jordan_steps(augmented)[:, m:]
    projected = direct - contract(inner, scale_col * solved, ((1,), (0,)))
    mixing = projected * weight
    o_ref[...] = x + contract(mixing, spread, ((0,), (0,)))


def analysis(flat, observed, fidelity, value, variance, noise):
    m = flat.shape[0]
    vmem = pl.BlockSpec(memory_space=pltpu.VMEM)
    return pl.pallas_call(
        analysis_kernel,
        out_shape=jax.ShapeDtypeStruct(flat.shape, jnp.float32),
        in_specs=[vmem] * 7,
        out_specs=vmem,
        compiler_params=pltpu.CompilerParams(vmem_limit_bytes=48 * 1024 * 1024),
    )(
        flat,
        observed,
        fidelity.reshape(m, 1),
        fidelity.reshape(1, m),
        value.reshape(1, -1),
        variance.reshape(1, -1),
        noise,
    )


def shifted(field, offset, axis):
    size = field.shape[axis]
    rolled = pltpu.roll(field, (-offset) % size, axis)
    place = lax.broadcasted_iota(jnp.int32, field.shape, axis) + offset
    return jnp.where((place >= 0) & (place < size), rolled, 0.0)


def kernel_neighbours(field):
    return (shifted(field, 1, 1), shifted(field, -1, 1), shifted(field, 1, 0), shifted(field, -1, 0))


def kernel_east(field):
    ahead, behind, upper, lower = kernel_neighbours(field)
    return 0.5 * (ahead - behind)


def kernel_north(field):
    ahead, behind, upper, lower = kernel_neighbours(field)
    return 0.5 * (upper - lower)


def kernel_laplace(field):
    ahead, behind, upper, lower = kernel_neighbours(field)
    return ahead + behind + upper + lower - 4.0 * field


def forecast_kernel(fid_ref, x_ref, o_ref):
    members, _, lat_rows, _ = x_ref.shape
    row = lax.broadcasted_iota(jnp.int32, (lat_rows, 1), 0).astype(jnp.float32)
    coriolis = 0.1 + 0.2 * (row + 0.5) / lat_rows
    for member in range(members):
        level = fid_ref[member]
        nonlinear = jnp.where(level == 0, 1.0, 0.0).astype(jnp.float32)
        friction = jnp.where(level == 0, 0.0, slow_friction).astype(jnp.float32)
        height, eastward, northward = x_ref[member, 0], x_ref[member, 1], x_ref[member, 2]
        for step in range(PREDICTION_COUNT):
            depth = 1.0 + nonlinear * height
            height_new = (
                height
                - time_step * (kernel_east(depth * eastward) + kernel_north(depth * northward))
                + time_step * viscous * kernel_laplace(height)
            )
            east_new = eastward + time_step * (
                -nonlinear * (eastward * kernel_east(eastward) + northward * kernel_north(eastward))
                + coriolis * northward
                - kernel_east(height_new)
                + viscous * kernel_laplace(eastward)
                - friction * eastward
            )
            north_new = northward + time_step * (
                -nonlinear * (eastward * kernel_east(northward) + northward * kernel_north(northward))
                - coriolis * eastward
                - kernel_north(height_new)
                + viscous * kernel_laplace(northward)
                - friction * northward
            )
            height, eastward, northward = height_new, east_new, north_new
        o_ref[member, 0] = height
        o_ref[member, 1] = eastward
        o_ref[member, 2] = northward


def forecast(initial, levels):
    return pl.pallas_call(
        forecast_kernel,
        out_shape=jax.ShapeDtypeStruct(initial.shape, jnp.float32),
        in_specs=[
            pl.BlockSpec(memory_space=pltpu.SMEM),
            pl.BlockSpec(memory_space=pltpu.VMEM),
        ],
        out_specs=pl.BlockSpec(memory_space=pltpu.VMEM),
    )(levels, initial)


def shards(initial_height_velocity, member_fidelity, obs_cell, obs_value, obs_var, obs_noise):
    per_device = initial_height_velocity.shape[0]
    resident_realizations = lax.dynamic_slice_in_dim(
        member_fidelity, lax.axis_index("band") * per_device, per_device
    )
    integrate_realizations = forecast(initial_height_velocity, resident_realizations)
    tile_worker = lax.all_to_all(
        integrate_realizations, "band", split_axis=2, concat_axis=0, tiled=True
    )
    ensemble_members = tile_worker.shape[0]
    tile_rows = tile_worker.shape[2]
    flat = tile_worker.reshape(ensemble_members, -1)
    block = extended(tile_worker, (("band", 2),), tile_rows)
    observed = jnp.take(block.reshape(ensemble_members, -1), obs_cell[0], axis=1)
    result = analysis(
        flat,
        observed,
        member_fidelity,
        obs_value[0],
        obs_var[0],
        obs_noise[0],
    ).reshape(tile_worker.shape)
    return lax.all_to_all(result, "band", split_axis=0, concat_axis=2, tiled=True)


def solution(mesh):
    in_specs = (
        P(("groups", "band"), None, None, None),
        P("groups"),
        P(("groups", "band"), None),
        P(("groups", "band"), None),
        P(("groups", "band"), None),
        P(("groups", "band"), None, None),
    )
    out_specs = P(("groups", "band"), None, None, None)
    return jax.shard_map(shards, mesh=mesh, in_specs=in_specs, out_specs=out_specs, check_vma=False)
```

```python
import jax
import jax.numpy as jnp
from jax import lax
from jax.sharding import PartitionSpec as P
from jax.experimental import pallas as pl
from jax.experimental.pallas import tpu as pltpu

PREDICTION_COUNT = 4


exact = lax.Precision.HIGHEST
time_step = 0.25
viscous = 0.05
slow_friction = 0.2
control_weight = 0.5


def extended(shard, sides, width):
    for axis, dim in sides:
        devices, length = (lax.axis_size(axis), shard.shape[dim])
        up = [(i, (i + 1) % devices) for i in range(devices - 1)]
        down = [(j, i) for i, j in up]
        last = lax.slice_in_dim(shard, length - width, length, axis=dim)
        leading = lax.slice_in_dim(shard, 0, width, axis=dim)
        before = lax.ppermute(last, axis, up)
        after = lax.ppermute(leading, axis, down)
        shard = jnp.concatenate([before, shard, after], axis=dim)
    return shard


def neighbours(field):
    lon_pad = jnp.pad(field, [(0, 0)] * (field.ndim - 1) + [(1, 1)])
    lat_pad = jnp.pad(field, [(0, 0)] * (field.ndim - 2) + [(1, 1), (0, 0)])
    return (lon_pad[..., 2:], lon_pad[..., :-2], lat_pad[..., 2:, :], lat_pad[..., :-2, :])


def east_slope(field):
    ahead, behind, upper, lower = neighbours(field)
    return 0.5 * (ahead - behind)


def north_slope(field):
    ahead, behind, upper, lower = neighbours(field)
    return 0.5 * (upper - lower)


def laplace(field):
    ahead, behind, upper, lower = neighbours(field)
    return ahead + behind + upper + lower - 4.0 * field


def advance(height, eastward, northward, nonlinear, friction, coriolis):
    depth = 1.0 + nonlinear * height
    height_new = (
        height
        - time_step * (east_slope(depth * eastward) + north_slope(depth * northward))
        + time_step * viscous * laplace(height)
    )
    east_new = eastward + time_step * (
        -nonlinear * (eastward * east_slope(eastward) + northward * north_slope(eastward))
        + coriolis * northward
        - east_slope(height_new)
        + viscous * laplace(eastward)
        - friction * eastward
    )
    north_new = northward + time_step * (
        -nonlinear * (eastward * east_slope(northward) + northward * north_slope(northward))
        - coriolis * eastward
        - north_slope(height_new)
        + viscous * laplace(northward)
        - friction * northward
    )
    return (height_new, east_new, north_new)


def begin_prediction(marine_condition, accuracy_levels, realization_count):
    nonlinear = (accuracy_levels == 0).astype(jnp.float32)[:, None, None]
    friction = jnp.where(accuracy_levels == 0, 0.0, slow_friction).astype(jnp.float32)[
        :, None, None
    ]
    lat_rows = marine_condition.shape[2]
    coriolis = (0.1 + 0.2 * (jnp.arange(lat_rows).astype(jnp.float32) + 0.5) / lat_rows)[:, None]
    height, eastward, northward = (
        marine_condition[:, 0],
        marine_condition[:, 1],
        marine_condition[:, 2],
    )
    for step in range(realization_count):
        height, eastward, northward = advance(
            height, eastward, northward, nonlinear, friction, coriolis
        )
    return jnp.stack([height, eastward, northward], axis=1)


def class_tables(accuracy_levels):
    onehot = (accuracy_levels[:, None] == jnp.arange(3)[None, :]).astype(jnp.float32)
    counts = jnp.sum(onehot, axis=0)
    coefs = jnp.stack(
        [
            1.0 / (counts[0] - 1.0),
            -control_weight / (counts[1] - 1.0),
            control_weight / (counts[2] - 1.0),
        ]
    )
    member_weight = jnp.sum(onehot * coefs[None, :], axis=1)
    return (onehot, counts, member_weight)


def remove_means(data, onehot, counts):
    means = jnp.dot(onehot.T, data, precision=exact) / counts[:, None]
    return data - jnp.dot(onehot, means, precision=exact)


def spd_solve(factor, rhs):
    inner = lax.linalg.triangular_solve(factor, rhs, left_side=True, lower=True)
    return lax.linalg.triangular_solve(factor, inner, left_side=True, lower=True, transpose_a=True)


def gauss_jordan_steps(a):
    n = a.shape[0]
    lane = lax.broadcasted_iota(jnp.int32, a.shape, 1)
    row_id = lax.broadcasted_iota(jnp.int32, (n, 1), 0)
    if n <= 64:
        for k in range(n):
            pivot_row = a[k : k + 1, :] * (1.0 / a[k : k + 1, k : k + 1])
            column = a[:, k : k + 1] - (row_id == k).astype(jnp.float32)
            a = a - column * pivot_row
        return a

    def step(k, a):
        pivot_row = jnp.sum(jnp.where(row_id == k, a, 0.0), axis=0, keepdims=True)
        column = jnp.sum(jnp.where(lane == k, a, 0.0), axis=1, keepdims=True)
        pivot = jnp.sum(jnp.where(lane[0:1] == k, pivot_row, 0.0), axis=1, keepdims=True)
        pivot_row = pivot_row / pivot
        column = column - (row_id == k).astype(jnp.float32)
        return a - column * pivot_row

    return lax.fori_loop(0, n, step, a)

def contract(a, b, dims):
    return lax.dot_general(
        a, b, (dims, ((), ())), precision=exact, preferred_element_type=jnp.float32
    )


def analysis_kernel(x_ref, ob_ref, fid_col_ref, fid_row_ref, value_ref, var_ref, noise_ref, o_ref):
    per_device = fid_col_ref.shape[1]
    width = x_ref.shape[1] // per_device
    x = jnp.concatenate([x_ref[:, i * width : (i + 1) * width] for i in range(per_device)], axis=0)
    m = x.shape[0]
    ob = ob_ref[...]
    fid_col = jnp.concatenate([fid_col_ref[:, i : i + 1] for i in range(per_device)], axis=0)
    fid_row = jnp.concatenate([fid_row_ref[i : i + 1, :] for i in range(per_device)], axis=1)
    variance = var_ref[...]
    masks = [(fid_col == c).astype(jnp.float32) for c in range(3)]
    masks_row = [(fid_row == c).astype(jnp.float32) for c in range(3)]
    counts = [jnp.sum(mask, axis=0, keepdims=True) for mask in masks]

    def remove_means(data):
        centred = data
        for mask, count in zip(masks, counts):
            centred = centred - mask * (jnp.sum(mask * data, axis=0, keepdims=True) / count)
        return centred

    spread = remove_means(x)
    obs_spread = remove_means(ob)
    weight = (
        masks[0] * (1.0 / (counts[0] - 1.0))
        + masks[1] * (-control_weight / (counts[1] - 1.0))
        + masks[2] * (control_weight / (counts[2] - 1.0))
    )
    scale_col = jnp.sqrt(masks[0] / (counts[0] - 1.0))
    count_row = jnp.sum(masks_row[0], axis=1, keepdims=True)
    scale_row = jnp.sqrt(masks_row[0] / (count_row - 1.0))
    weighted = obs_spread / variance
    inner = contract(weighted, obs_spread, ((1,), (1,)))
    direct = (
        jnp.sum(weighted * value_ref[...], axis=1, keepdims=True)
        + contract(weighted * jnp.sqrt(variance), noise_ref[...], ((1,), (0,)))
        - contract(weighted, ob, ((1,), (1,)))
    )
    row_id = lax.broadcasted_iota(jnp.int32, (m, m), 0)
    col_id = lax.broadcasted_iota(jnp.int32, (m, m), 1)
    system = (row_id == col_id).astype(jnp.float32) + scale_col * inner * scale_row
    augmented = jnp.concatenate([system, scale_col * direct], axis=1)
    solved = gauss_jordan_steps(augmented)[:, m:]
    projected = direct - contract(inner, scale_col * solved, ((1,), (0,)))
    mixing = projected * weight
    result = x + contract(mixing, spread, ((0,), (0,)))
    sources = x_ref.shape[0]
    for i in range(per_device):
        o_ref[:, i * width : (i + 1) * width] = result[i * sources : (i + 1) * sources]


def analysis(rows, observed, fidelity, value, variance, noise):
    sources = rows.shape[0]
    vmem = pl.BlockSpec(memory_space=pltpu.VMEM)
    return pl.pallas_call(
        analysis_kernel,
        out_shape=jax.ShapeDtypeStruct(rows.shape, jnp.float32),
        in_specs=[vmem] * 7,
        out_specs=vmem,
        compiler_params=pltpu.CompilerParams(vmem_limit_bytes=48 * 1024 * 1024),
    )(
        rows,
        observed,
        fidelity.reshape(sources, -1),
        fidelity.reshape(sources, -1).T,
        value.reshape(1, -1),
        variance.reshape(1, -1),
        noise,
    )


def shifted(field, offset, axis):
    size = field.shape[axis]
    rolled = pltpu.roll(field, (-offset) % size, axis)
    place = lax.broadcasted_iota(jnp.int32, field.shape, axis) + offset
    return jnp.where((place >= 0) & (place < size), rolled, 0.0)


def kernel_neighbours(field):
    return (shifted(field, 1, 1), shifted(field, -1, 1), shifted(field, 1, 0), shifted(field, -1, 0))


def kernel_east(field):
    ahead, behind, upper, lower = kernel_neighbours(field)
    return 0.5 * (ahead - behind)


def kernel_north(field):
    ahead, behind, upper, lower = kernel_neighbours(field)
    return 0.5 * (upper - lower)


def kernel_laplace(field):
    ahead, behind, upper, lower = kernel_neighbours(field)
    return ahead + behind + upper + lower - 4.0 * field


def forecast_kernel(fid_ref, x_ref, o_ref):
    members, _, lat_rows, lon = x_ref.shape
    first = lax.axis_index("band") * members
    row = lax.broadcasted_iota(jnp.int32, (lat_rows, 1), 0).astype(jnp.float32)
    coriolis = 0.1 + 0.2 * (row + 0.5) / lat_rows
    for member in range(members):
        level = fid_ref[first + member]
        nonlinear = jnp.where(level == 0, 1.0, 0.0).astype(jnp.float32)
        friction = jnp.where(level == 0, 0.0, slow_friction).astype(jnp.float32)
        height, eastward, northward = x_ref[member, 0], x_ref[member, 1], x_ref[member, 2]
        for step in range(PREDICTION_COUNT):
            depth = 1.0 + nonlinear * height
            height_new = (
                height
                - time_step * (kernel_east(depth * eastward) + kernel_north(depth * northward))
                + time_step * viscous * kernel_laplace(height)
            )
            east_new = eastward + time_step * (
                -nonlinear * (eastward * kernel_east(eastward) + northward * kernel_north(eastward))
                + coriolis * northward
                - kernel_east(height_new)
                + viscous * kernel_laplace(eastward)
                - friction * eastward
            )
            north_new = northward + time_step * (
                -nonlinear * (eastward * kernel_east(northward) + northward * kernel_north(northward))
                - coriolis * eastward
                - kernel_north(height_new)
                + viscous * kernel_laplace(northward)
                - friction * northward
            )
            height, eastward, northward = height_new, east_new, north_new
        for component, field in enumerate((height, eastward, northward)):
            o_ref[:, pl.ds((member * 3 + component) * lon, lon)] = field


def forecast(initial, levels):
    members, components, lat_rows, lon = initial.shape
    return pl.pallas_call(
        forecast_kernel,
        out_shape=jax.ShapeDtypeStruct((lat_rows, members * components * lon), jnp.float32),
        in_specs=[
            pl.BlockSpec(memory_space=pltpu.SMEM),
            pl.BlockSpec(memory_space=pltpu.VMEM),
        ],
        out_specs=pl.BlockSpec(memory_space=pltpu.VMEM),
    )(levels, initial)


def shards(initial_height_velocity, member_fidelity, obs_cell, obs_value, obs_var, obs_noise):
    per_device, components, lat_rows, lon = initial_height_velocity.shape
    sources = lax.axis_size("band")
    rows = forecast(initial_height_velocity, member_fidelity)
    rows = lax.all_to_all(rows, "band", 0, 0, tiled=True)
    up = [(i, i + 1) for i in range(sources - 1)]
    down = [(j, i) for i, j in up]
    below = lax.ppermute(rows, "band", up)
    above = lax.ppermute(rows, "band", down)
    block = jnp.stack([below, rows, above]).reshape(3, sources, per_device, components, lon)
    block = jnp.transpose(block, (2, 1, 3, 0, 4)).reshape(sources * per_device, -1)
    observed = jnp.take(block, obs_cell[0], axis=1)
    noise = obs_noise[0].reshape(-1, sources, per_device)
    noise = jnp.transpose(noise, (0, 2, 1)).reshape(-1, sources * per_device)
    result = analysis(rows, observed, member_fidelity, obs_value[0], obs_var[0], noise)
    result = lax.all_to_all(result, "band", 0, 0, tiled=True)
    result = result.reshape(lat_rows, per_device, components, lon)
    return jnp.transpose(result, (1, 2, 0, 3))


def solution(mesh):
    in_specs = (
        P(("groups", "band"), None, None, None),
        P("groups"),
        P(("groups", "band"), None),
        P(("groups", "band"), None),
        P(("groups", "band"), None),
        P(("groups", "band"), None, None),
    )
    out_specs = P(("groups", "band"), None, None, None)
    return jax.shard_map(shards, mesh=mesh, in_specs=in_specs, out_specs=out_specs, check_vma=False)
```

```python
import jax
import jax.numpy as jnp
from jax import lax
from jax.sharding import PartitionSpec as P
from jax.experimental import pallas as pl
from jax.experimental.pallas import tpu as pltpu

PREDICTION_COUNT = 4


exact = lax.Precision.HIGHEST
time_step = 0.25
viscous = 0.05
slow_friction = 0.2
control_weight = 0.5


def extended(shard, sides, width):
    for axis, dim in sides:
        devices, length = (lax.axis_size(axis), shard.shape[dim])
        up = [(i, (i + 1) % devices) for i in range(devices - 1)]
        down = [(j, i) for i, j in up]
        last = lax.slice_in_dim(shard, length - width, length, axis=dim)
        leading = lax.slice_in_dim(shard, 0, width, axis=dim)
        before = lax.ppermute(last, axis, up)
        after = lax.ppermute(leading, axis, down)
        shard = jnp.concatenate([before, shard, after], axis=dim)
    return shard


def neighbours(field):
    lon_pad = jnp.pad(field, [(0, 0)] * (field.ndim - 1) + [(1, 1)])
    lat_pad = jnp.pad(field, [(0, 0)] * (field.ndim - 2) + [(1, 1), (0, 0)])
    return (lon_pad[..., 2:], lon_pad[..., :-2], lat_pad[..., 2:, :], lat_pad[..., :-2, :])


def east_slope(field):
    ahead, behind, upper, lower = neighbours(field)
    return 0.5 * (ahead - behind)


def north_slope(field):
    ahead, behind, upper, lower = neighbours(field)
    return 0.5 * (upper - lower)


def laplace(field):
    ahead, behind, upper, lower = neighbours(field)
    return ahead + behind + upper + lower - 4.0 * field


def advance(height, eastward, northward, nonlinear, friction, coriolis):
    depth = 1.0 + nonlinear * height
    height_new = (
        height
        - time_step * (east_slope(depth * eastward) + north_slope(depth * northward))
        + time_step * viscous * laplace(height)
    )
    east_new = eastward + time_step * (
        -nonlinear * (eastward * east_slope(eastward) + northward * north_slope(eastward))
        + coriolis * northward
        - east_slope(height_new)
        + viscous * laplace(eastward)
        - friction * eastward
    )
    north_new = northward + time_step * (
        -nonlinear * (eastward * east_slope(northward) + northward * north_slope(northward))
        - coriolis * eastward
        - north_slope(height_new)
        + viscous * laplace(northward)
        - friction * northward
    )
    return (height_new, east_new, north_new)


def begin_prediction(marine_condition, accuracy_levels, realization_count):
    nonlinear = (accuracy_levels == 0).astype(jnp.float32)[:, None, None]
    friction = jnp.where(accuracy_levels == 0, 0.0, slow_friction).astype(jnp.float32)[
        :, None, None
    ]
    lat_rows = marine_condition.shape[2]
    coriolis = (0.1 + 0.2 * (jnp.arange(lat_rows).astype(jnp.float32) + 0.5) / lat_rows)[:, None]
    height, eastward, northward = (
        marine_condition[:, 0],
        marine_condition[:, 1],
        marine_condition[:, 2],
    )
    for step in range(realization_count):
        height, eastward, northward = advance(
            height, eastward, northward, nonlinear, friction, coriolis
        )
    return jnp.stack([height, eastward, northward], axis=1)


def class_tables(accuracy_levels):
    onehot = (accuracy_levels[:, None] == jnp.arange(3)[None, :]).astype(jnp.float32)
    counts = jnp.sum(onehot, axis=0)
    coefs = jnp.stack(
        [
            1.0 / (counts[0] - 1.0),
            -control_weight / (counts[1] - 1.0),
            control_weight / (counts[2] - 1.0),
        ]
    )
    member_weight = jnp.sum(onehot * coefs[None, :], axis=1)
    return (onehot, counts, member_weight)


def remove_means(data, onehot, counts):
    means = jnp.dot(onehot.T, data, precision=exact) / counts[:, None]
    return data - jnp.dot(onehot, means, precision=exact)


def spd_solve(factor, rhs):
    inner = lax.linalg.triangular_solve(factor, rhs, left_side=True, lower=True)
    return lax.linalg.triangular_solve(factor, inner, left_side=True, lower=True, transpose_a=True)


def gauss_jordan_steps(a):
    n = a.shape[0]
    lane = lax.broadcasted_iota(jnp.int32, a.shape, 1)
    row_id = lax.broadcasted_iota(jnp.int32, (n, 1), 0)
    if n <= 64:
        for k in range(n):
            pivot_row = a[k : k + 1, :] * (1.0 / a[k : k + 1, k : k + 1])
            column = a[:, k : k + 1] - (row_id == k).astype(jnp.float32)
            a = a - column * pivot_row
        return a

    def step(k, a):
        pivot_row = jnp.sum(jnp.where(row_id == k, a, 0.0), axis=0, keepdims=True)
        column = jnp.sum(jnp.where(lane == k, a, 0.0), axis=1, keepdims=True)
        pivot = jnp.sum(jnp.where(lane[0:1] == k, pivot_row, 0.0), axis=1, keepdims=True)
        pivot_row = pivot_row / pivot
        column = column - (row_id == k).astype(jnp.float32)
        return a - column * pivot_row

    return lax.fori_loop(0, n, step, a)

def contract(a, b, dims):
    return lax.dot_general(
        a, b, (dims, ((), ())), precision=exact, preferred_element_type=jnp.float32
    )


def analysis_kernel(x_ref, ob_ref, fid_col_ref, fid_row_ref, value_ref, var_ref, noise_ref, o_ref):
    per_device = fid_col_ref.shape[1]
    width = x_ref.shape[2] // per_device
    x = jnp.concatenate([x_ref[:, 0, i * width : (i + 1) * width] for i in range(per_device)], axis=0)
    m = x.shape[0]
    ob = ob_ref[...]
    fid_col = jnp.concatenate([fid_col_ref[:, i : i + 1] for i in range(per_device)], axis=0)
    fid_row = jnp.concatenate([fid_row_ref[i : i + 1, :] for i in range(per_device)], axis=1)
    variance = var_ref[...]
    masks = [(fid_col == c).astype(jnp.float32) for c in range(3)]
    masks_row = [(fid_row == c).astype(jnp.float32) for c in range(3)]
    counts = [jnp.sum(mask, axis=0, keepdims=True) for mask in masks]

    def remove_means(data):
        centred = data
        for mask, count in zip(masks, counts):
            centred = centred - mask * (jnp.sum(mask * data, axis=0, keepdims=True) / count)
        return centred

    spread = remove_means(x)
    obs_spread = remove_means(ob)
    weight = (
        masks[0] * (1.0 / (counts[0] - 1.0))
        + masks[1] * (-control_weight / (counts[1] - 1.0))
        + masks[2] * (control_weight / (counts[2] - 1.0))
    )
    scale_col = jnp.sqrt(masks[0] / (counts[0] - 1.0))
    count_row = jnp.sum(masks_row[0], axis=1, keepdims=True)
    scale_row = jnp.sqrt(masks_row[0] / (count_row - 1.0))
    weighted = obs_spread / variance
    inner = contract(weighted, obs_spread, ((1,), (1,)))
    direct = (
        jnp.sum(weighted * value_ref[...], axis=1, keepdims=True)
        + contract(weighted * jnp.sqrt(variance), noise_ref[...], ((1,), (0,)))
        - contract(weighted, ob, ((1,), (1,)))
    )
    row_id = lax.broadcasted_iota(jnp.int32, (m, m), 0)
    col_id = lax.broadcasted_iota(jnp.int32, (m, m), 1)
    system = (row_id == col_id).astype(jnp.float32) + scale_col * inner * scale_row
    augmented = jnp.concatenate([system, scale_col * direct], axis=1)
    solved = gauss_jordan_steps(augmented)[:, m:]
    projected = direct - contract(inner, scale_col * solved, ((1,), (0,)))
    mixing = projected * weight
    result = x + contract(mixing, spread, ((0,), (0,)))
    sources = x_ref.shape[0]
    for i in range(per_device):
        o_ref[:, 0, i * width : (i + 1) * width] = result[i * sources : (i + 1) * sources]


def analysis(rows, observed, fidelity, value, variance, noise):
    sources = rows.shape[0]
    vmem = pl.BlockSpec(memory_space=pltpu.VMEM)
    return pl.pallas_call(
        analysis_kernel,
        out_shape=jax.ShapeDtypeStruct(rows.shape, jnp.float32),
        in_specs=[vmem] * 7,
        out_specs=vmem,
        compiler_params=pltpu.CompilerParams(vmem_limit_bytes=48 * 1024 * 1024),
    )(
        rows,
        observed,
        fidelity.reshape(sources, -1),
        fidelity.reshape(sources, -1).T,
        value.reshape(1, -1),
        variance.reshape(1, -1),
        noise,
    )


def shifted(field, offset, axis):
    size = field.shape[axis]
    rolled = pltpu.roll(field, (-offset) % size, axis)
    place = lax.broadcasted_iota(jnp.int32, field.shape, axis) + offset
    return jnp.where((place >= 0) & (place < size), rolled, 0.0)


def kernel_neighbours(field):
    return (shifted(field, 1, 1), shifted(field, -1, 1), shifted(field, 1, 0), shifted(field, -1, 0))


def kernel_east(field):
    ahead, behind, upper, lower = kernel_neighbours(field)
    return 0.5 * (ahead - behind)


def kernel_north(field):
    ahead, behind, upper, lower = kernel_neighbours(field)
    return 0.5 * (upper - lower)


def kernel_laplace(field):
    ahead, behind, upper, lower = kernel_neighbours(field)
    return ahead + behind + upper + lower - 4.0 * field


def forecast_kernel(fid_ref, x_ref, o_ref):
    members, _, lat_rows, lon = x_ref.shape
    first = lax.axis_index("band") * members
    row = lax.broadcasted_iota(jnp.int32, (lat_rows, 1), 0).astype(jnp.float32)
    coriolis = 0.1 + 0.2 * (row + 0.5) / lat_rows
    for member in range(members):
        level = fid_ref[first + member]
        nonlinear = jnp.where(level == 0, 1.0, 0.0).astype(jnp.float32)
        friction = jnp.where(level == 0, 0.0, slow_friction).astype(jnp.float32)
        height, eastward, northward = x_ref[member, 0], x_ref[member, 1], x_ref[member, 2]
        for step in range(PREDICTION_COUNT):
            depth = 1.0 + nonlinear * height
            height_new = (
                height
                - time_step * (kernel_east(depth * eastward) + kernel_north(depth * northward))
                + time_step * viscous * kernel_laplace(height)
            )
            east_new = eastward + time_step * (
                -nonlinear * (eastward * kernel_east(eastward) + northward * kernel_north(eastward))
                + coriolis * northward
                - kernel_east(height_new)
                + viscous * kernel_laplace(eastward)
                - friction * eastward
            )
            north_new = northward + time_step * (
                -nonlinear * (eastward * kernel_east(northward) + northward * kernel_north(northward))
                - coriolis * eastward
                - kernel_north(height_new)
                + viscous * kernel_laplace(northward)
                - friction * northward
            )
            height, eastward, northward = height_new, east_new, north_new
        for component, field in enumerate((height, eastward, northward)):
            o_ref[:, 0, pl.ds((member * 3 + component) * lon, lon)] = field


def forecast(initial, levels):
    members, components, lat_rows, lon = initial.shape
    return pl.pallas_call(
        forecast_kernel,
        out_shape=jax.ShapeDtypeStruct((lat_rows, 1, members * components * lon), jnp.float32),
        in_specs=[
            pl.BlockSpec(memory_space=pltpu.SMEM),
            pl.BlockSpec(memory_space=pltpu.VMEM),
        ],
        out_specs=pl.BlockSpec(memory_space=pltpu.VMEM),
    )(levels, initial)


def shards(initial_height_velocity, member_fidelity, obs_cell, obs_value, obs_var, obs_noise):
    per_device, components, lat_rows, lon = initial_height_velocity.shape
    sources = lax.axis_size("band")
    rows = forecast(initial_height_velocity, member_fidelity)
    rows = lax.all_to_all(rows, "band", 0, 0, tiled=True)
    up = [(i, i + 1) for i in range(sources - 1)]
    down = [(j, i) for i, j in up]
    below = lax.ppermute(rows, "band", up)
    above = lax.ppermute(rows, "band", down)
    block = jnp.concatenate([below, rows, above], axis=1).reshape(sources, 3, per_device, components, lon)
    block = jnp.transpose(block, (2, 0, 3, 1, 4)).reshape(sources * per_device, -1)
    observed = jnp.take(block, obs_cell[0], axis=1)
    noise = obs_noise[0].reshape(-1, sources, per_device)
    noise = jnp.transpose(noise, (0, 2, 1)).reshape(-1, sources * per_device)
    result = analysis(rows, observed, member_fidelity, obs_value[0], obs_var[0], noise)
    result = lax.all_to_all(result, "band", 0, 0, tiled=True)
    result = result.reshape(lat_rows, per_device, components, lon)
    return jnp.transpose(result, (1, 2, 0, 3))


def solution(mesh):
    in_specs = (
        P(("groups", "band"), None, None, None),
        P("groups"),
        P(("groups", "band"), None),
        P(("groups", "band"), None),
        P(("groups", "band"), None),
        P(("groups", "band"), None, None),
    )
    out_specs = P(("groups", "band"), None, None, None)
    return jax.shard_map(shards, mesh=mesh, in_specs=in_specs, out_specs=out_specs, check_vma=False)
```

```python
import jax
import jax.numpy as jnp
from jax import lax
from jax.sharding import PartitionSpec as P
from jax.experimental import pallas as pl
from jax.experimental.pallas import tpu as pltpu

PREDICTION_COUNT = 4


exact = lax.Precision.HIGHEST
time_step = 0.25
viscous = 0.05
slow_friction = 0.2
control_weight = 0.5


def extended(shard, sides, width):
    for axis, dim in sides:
        devices, length = (lax.axis_size(axis), shard.shape[dim])
        up = [(i, (i + 1) % devices) for i in range(devices - 1)]
        down = [(j, i) for i, j in up]
        last = lax.slice_in_dim(shard, length - width, length, axis=dim)
        leading = lax.slice_in_dim(shard, 0, width, axis=dim)
        before = lax.ppermute(last, axis, up)
        after = lax.ppermute(leading, axis, down)
        shard = jnp.concatenate([before, shard, after], axis=dim)
    return shard


def neighbours(field):
    lon_pad = jnp.pad(field, [(0, 0)] * (field.ndim - 1) + [(1, 1)])
    lat_pad = jnp.pad(field, [(0, 0)] * (field.ndim - 2) + [(1, 1), (0, 0)])
    return (lon_pad[..., 2:], lon_pad[..., :-2], lat_pad[..., 2:, :], lat_pad[..., :-2, :])


def east_slope(field):
    ahead, behind, upper, lower = neighbours(field)
    return 0.5 * (ahead - behind)


def north_slope(field):
    ahead, behind, upper, lower = neighbours(field)
    return 0.5 * (upper - lower)


def laplace(field):
    ahead, behind, upper, lower = neighbours(field)
    return ahead + behind + upper + lower - 4.0 * field


def advance(height, eastward, northward, nonlinear, friction, coriolis):
    depth = 1.0 + nonlinear * height
    height_new = (
        height
        - time_step * (east_slope(depth * eastward) + north_slope(depth * northward))
        + time_step * viscous * laplace(height)
    )
    east_new = eastward + time_step * (
        -nonlinear * (eastward * east_slope(eastward) + northward * north_slope(eastward))
        + coriolis * northward
        - east_slope(height_new)
        + viscous * laplace(eastward)
        - friction * eastward
    )
    north_new = northward + time_step * (
        -nonlinear * (eastward * east_slope(northward) + northward * north_slope(northward))
        - coriolis * eastward
        - north_slope(height_new)
        + viscous * laplace(northward)
        - friction * northward
    )
    return (height_new, east_new, north_new)


def begin_prediction(marine_condition, accuracy_levels, realization_count):
    nonlinear = (accuracy_levels == 0).astype(jnp.float32)[:, None, None]
    friction = jnp.where(accuracy_levels == 0, 0.0, slow_friction).astype(jnp.float32)[
        :, None, None
    ]
    lat_rows = marine_condition.shape[2]
    coriolis = (0.1 + 0.2 * (jnp.arange(lat_rows).astype(jnp.float32) + 0.5) / lat_rows)[:, None]
    height, eastward, northward = (
        marine_condition[:, 0],
        marine_condition[:, 1],
        marine_condition[:, 2],
    )
    for step in range(realization_count):
        height, eastward, northward = advance(
            height, eastward, northward, nonlinear, friction, coriolis
        )
    return jnp.stack([height, eastward, northward], axis=1)


def class_tables(accuracy_levels):
    onehot = (accuracy_levels[:, None] == jnp.arange(3)[None, :]).astype(jnp.float32)
    counts = jnp.sum(onehot, axis=0)
    coefs = jnp.stack(
        [
            1.0 / (counts[0] - 1.0),
            -control_weight / (counts[1] - 1.0),
            control_weight / (counts[2] - 1.0),
        ]
    )
    member_weight = jnp.sum(onehot * coefs[None, :], axis=1)
    return (onehot, counts, member_weight)


def remove_means(data, onehot, counts):
    means = jnp.dot(onehot.T, data, precision=exact) / counts[:, None]
    return data - jnp.dot(onehot, means, precision=exact)


def spd_solve(factor, rhs):
    inner = lax.linalg.triangular_solve(factor, rhs, left_side=True, lower=True)
    return lax.linalg.triangular_solve(factor, inner, left_side=True, lower=True, transpose_a=True)


def gauss_jordan_steps(a):
    n = a.shape[0]
    lane = lax.broadcasted_iota(jnp.int32, a.shape, 1)
    row_id = lax.broadcasted_iota(jnp.int32, (n, 1), 0)
    if n <= 64:
        for k in range(n):
            pivot_row = a[k : k + 1, :] * (1.0 / a[k : k + 1, k : k + 1])
            column = a[:, k : k + 1] - (row_id == k).astype(jnp.float32)
            a = a - column * pivot_row
        return a

    def step(k, a):
        pivot_row = jnp.sum(jnp.where(row_id == k, a, 0.0), axis=0, keepdims=True)
        column = jnp.sum(jnp.where(lane == k, a, 0.0), axis=1, keepdims=True)
        pivot = jnp.sum(jnp.where(lane[0:1] == k, pivot_row, 0.0), axis=1, keepdims=True)
        pivot_row = pivot_row / pivot
        column = column - (row_id == k).astype(jnp.float32)
        return a - column * pivot_row

    return lax.fori_loop(0, n, step, a)

def contract(a, b, dims):
    return lax.dot_general(
        a, b, (dims, ((), ())), precision=exact, preferred_element_type=jnp.float32
    )


def analysis_kernel(x_ref, ob_ref, fid_col_ref, fid_row_ref, value_ref, var_ref, noise_ref, o_ref):
    per_device = fid_col_ref.shape[1]
    width = x_ref.shape[2] // per_device
    x = jnp.concatenate([x_ref[:, 0, i * width : (i + 1) * width] for i in range(per_device)], axis=0)
    m = x.shape[0]
    ob = ob_ref[...]
    fid_col = jnp.concatenate([fid_col_ref[:, i : i + 1] for i in range(per_device)], axis=0)
    fid_row = jnp.concatenate([fid_row_ref[i : i + 1, :] for i in range(per_device)], axis=1)
    variance = var_ref[...]
    masks = [(fid_col == c).astype(jnp.float32) for c in range(3)]
    masks_row = [(fid_row == c).astype(jnp.float32) for c in range(3)]
    counts = [jnp.sum(mask, axis=0, keepdims=True) for mask in masks]

    def remove_means(data):
        centred = data
        for mask, count in zip(masks, counts):
            centred = centred - mask * (jnp.sum(mask * data, axis=0, keepdims=True) / count)
        return centred

    spread = remove_means(x)
    obs_spread = remove_means(ob)
    weight = (
        masks[0] * (1.0 / (counts[0] - 1.0))
        + masks[1] * (-control_weight / (counts[1] - 1.0))
        + masks[2] * (control_weight / (counts[2] - 1.0))
    )
    scale_col = jnp.sqrt(masks[0] / (counts[0] - 1.0))
    count_row = jnp.sum(masks_row[0], axis=1, keepdims=True)
    scale_row = jnp.sqrt(masks_row[0] / (count_row - 1.0))
    weighted = obs_spread / variance
    inner = contract(weighted, obs_spread, ((1,), (1,)))
    direct = (
        jnp.sum(weighted * value_ref[...], axis=1, keepdims=True)
        + contract(weighted * jnp.sqrt(variance), noise_ref[...], ((1,), (0,)))
        - contract(weighted, ob, ((1,), (1,)))
    )
    row_id = lax.broadcasted_iota(jnp.int32, (m, m), 0)
    col_id = lax.broadcasted_iota(jnp.int32, (m, m), 1)
    system = (row_id == col_id).astype(jnp.float32) + scale_col * inner * scale_row
    augmented = jnp.concatenate([system, scale_col * direct], axis=1)
    solved = gauss_jordan_steps(augmented)[:, m:]
    projected = direct - contract(inner, scale_col * solved, ((1,), (0,)))
    mixing = projected * weight
    result = x + contract(mixing, spread, ((0,), (0,)))
    sources = x_ref.shape[0]
    for i in range(per_device):
        o_ref[:, 0, i * width : (i + 1) * width] = result[i * sources : (i + 1) * sources]


def analysis(rows, observed, fidelity, value, variance, noise):
    sources = rows.shape[0]
    vmem = pl.BlockSpec(memory_space=pltpu.VMEM)
    return pl.pallas_call(
        analysis_kernel,
        out_shape=jax.ShapeDtypeStruct(rows.shape, jnp.float32),
        in_specs=[vmem] * 7,
        out_specs=vmem,
        compiler_params=pltpu.CompilerParams(vmem_limit_bytes=48 * 1024 * 1024),
    )(
        rows,
        observed,
        fidelity.reshape(sources, -1),
        fidelity.reshape(sources, -1).T,
        value.reshape(1, -1),
        variance.reshape(1, -1),
        noise,
    )


def shifted(field, offset, axis):
    size = field.shape[axis]
    rolled = pltpu.roll(field, (-offset) % size, axis)
    place = lax.broadcasted_iota(jnp.int32, field.shape, axis) + offset
    return jnp.where((place >= 0) & (place < size), rolled, 0.0)


def kernel_neighbours(field):
    return (shifted(field, 1, 1), shifted(field, -1, 1), shifted(field, 1, 0), shifted(field, -1, 0))


def kernel_east(field):
    ahead, behind, upper, lower = kernel_neighbours(field)
    return 0.5 * (ahead - behind)


def kernel_north(field):
    ahead, behind, upper, lower = kernel_neighbours(field)
    return 0.5 * (upper - lower)


def kernel_laplace(field):
    ahead, behind, upper, lower = kernel_neighbours(field)
    return ahead + behind + upper + lower - 4.0 * field


def forecast_kernel(fid_ref, x_ref, o_ref):
    members, _, lat_rows, lon = x_ref.shape
    first = lax.axis_index("band") * members
    row = lax.broadcasted_iota(jnp.int32, (lat_rows, 1), 0).astype(jnp.float32)
    coriolis = 0.1 + 0.2 * (row + 0.5) / lat_rows
    for member in range(members):
        level = fid_ref[first + member]
        nonlinear = jnp.where(level == 0, 1.0, 0.0).astype(jnp.float32)
        friction = jnp.where(level == 0, 0.0, slow_friction).astype(jnp.float32)
        height, eastward, northward = x_ref[member, 0], x_ref[member, 1], x_ref[member, 2]
        for step in range(PREDICTION_COUNT):
            depth = 1.0 + nonlinear * height
            height_new = (
                height
                - time_step * (kernel_east(depth * eastward) + kernel_north(depth * northward))
                + time_step * viscous * kernel_laplace(height)
            )
            east_new = eastward + time_step * (
                -nonlinear * (eastward * kernel_east(eastward) + northward * kernel_north(eastward))
                + coriolis * northward
                - kernel_east(height_new)
                + viscous * kernel_laplace(eastward)
                - friction * eastward
            )
            north_new = northward + time_step * (
                -nonlinear * (eastward * kernel_east(northward) + northward * kernel_north(northward))
                - coriolis * eastward
                - kernel_north(height_new)
                + viscous * kernel_laplace(northward)
                - friction * northward
            )
            height, eastward, northward = height_new, east_new, north_new
        for component, field in enumerate((height, eastward, northward)):
            o_ref[:, 0, pl.ds((member * 3 + component) * lon, lon)] = field


def forecast(initial, levels):
    members, components, lat_rows, lon = initial.shape
    return pl.pallas_call(
        forecast_kernel,
        out_shape=jax.ShapeDtypeStruct((lat_rows, 1, members * components * lon), jnp.float32),
        in_specs=[
            pl.BlockSpec(memory_space=pltpu.SMEM),
            pl.BlockSpec(memory_space=pltpu.VMEM),
        ],
        out_specs=pl.BlockSpec(memory_space=pltpu.VMEM),
    )(levels, initial)


def shards(initial_height_velocity, member_fidelity, obs_cell, obs_value, obs_var, obs_noise):
    per_device, components, lat_rows, lon = initial_height_velocity.shape
    sources = lax.axis_size("band")
    rows = forecast(initial_height_velocity, member_fidelity)
    rows = lax.all_to_all(rows, "band", 0, 0, tiled=True)
    up = [(i, i + 1) for i in range(sources - 1)]
    down = [(j, i) for i, j in up]
    below = lax.ppermute(rows, "band", up)
    above = lax.ppermute(rows, "band", down)
    block = jnp.concatenate([below, rows, above], axis=2).reshape(sources, -1)
    cells = obs_cell[0]
    component, place = cells // (3 * lon), cells % (3 * lon)
    offset, column = place // lon, place % lon
    width = per_device * components * lon
    picks = jnp.concatenate(
        [offset * width + (i * components + component) * lon + column for i in range(per_device)]
    )
    observed = jnp.take(block, picks, axis=1).reshape(sources, per_device, -1)
    observed = jnp.transpose(observed, (1, 0, 2)).reshape(sources * per_device, -1)
    noise = obs_noise[0].reshape(-1, sources, per_device)
    noise = jnp.transpose(noise, (0, 2, 1)).reshape(-1, sources * per_device)
    result = analysis(rows, observed, member_fidelity, obs_value[0], obs_var[0], noise)
    result = lax.all_to_all(result, "band", 0, 0, tiled=True)
    result = result.reshape(lat_rows, per_device, components, lon)
    return jnp.transpose(result, (1, 2, 0, 3))


def solution(mesh):
    in_specs = (
        P(("groups", "band"), None, None, None),
        P("groups"),
        P(("groups", "band"), None),
        P(("groups", "band"), None),
        P(("groups", "band"), None),
        P(("groups", "band"), None, None),
    )
    out_specs = P(("groups", "band"), None, None, None)
    return jax.shard_map(shards, mesh=mesh, in_specs=in_specs, out_specs=out_specs, check_vma=False)
```

```python
import jax
import jax.numpy as jnp
from jax import lax
from jax.sharding import PartitionSpec as P
from jax.experimental import pallas as pl
from jax.experimental.pallas import tpu as pltpu

PREDICTION_COUNT = 4


exact = lax.Precision.HIGHEST
time_step = 0.25
viscous = 0.05
slow_friction = 0.2
control_weight = 0.5


def extended(shard, sides, width):
    for axis, dim in sides:
        devices, length = (lax.axis_size(axis), shard.shape[dim])
        up = [(i, (i + 1) % devices) for i in range(devices - 1)]
        down = [(j, i) for i, j in up]
        last = lax.slice_in_dim(shard, length - width, length, axis=dim)
        leading = lax.slice_in_dim(shard, 0, width, axis=dim)
        before = lax.ppermute(last, axis, up)
        after = lax.ppermute(leading, axis, down)
        shard = jnp.concatenate([before, shard, after], axis=dim)
    return shard


def neighbours(field):
    lon_pad = jnp.pad(field, [(0, 0)] * (field.ndim - 1) + [(1, 1)])
    lat_pad = jnp.pad(field, [(0, 0)] * (field.ndim - 2) + [(1, 1), (0, 0)])
    return (lon_pad[..., 2:], lon_pad[..., :-2], lat_pad[..., 2:, :], lat_pad[..., :-2, :])


def east_slope(field):
    ahead, behind, upper, lower = neighbours(field)
    return 0.5 * (ahead - behind)


def north_slope(field):
    ahead, behind, upper, lower = neighbours(field)
    return 0.5 * (upper - lower)


def laplace(field):
    ahead, behind, upper, lower = neighbours(field)
    return ahead + behind + upper + lower - 4.0 * field


def advance(height, eastward, northward, nonlinear, friction, coriolis):
    depth = 1.0 + nonlinear * height
    height_new = (
        height
        - time_step * (east_slope(depth * eastward) + north_slope(depth * northward))
        + time_step * viscous * laplace(height)
    )
    east_new = eastward + time_step * (
        -nonlinear * (eastward * east_slope(eastward) + northward * north_slope(eastward))
        + coriolis * northward
        - east_slope(height_new)
        + viscous * laplace(eastward)
        - friction * eastward
    )
    north_new = northward + time_step * (
        -nonlinear * (eastward * east_slope(northward) + northward * north_slope(northward))
        - coriolis * eastward
        - north_slope(height_new)
        + viscous * laplace(northward)
        - friction * northward
    )
    return (height_new, east_new, north_new)


def begin_prediction(marine_condition, accuracy_levels, realization_count):
    nonlinear = (accuracy_levels == 0).astype(jnp.float32)[:, None, None]
    friction = jnp.where(accuracy_levels == 0, 0.0, slow_friction).astype(jnp.float32)[
        :, None, None
    ]
    lat_rows = marine_condition.shape[2]
    coriolis = (0.1 + 0.2 * (jnp.arange(lat_rows).astype(jnp.float32) + 0.5) / lat_rows)[:, None]
    height, eastward, northward = (
        marine_condition[:, 0],
        marine_condition[:, 1],
        marine_condition[:, 2],
    )
    for step in range(realization_count):
        height, eastward, northward = advance(
            height, eastward, northward, nonlinear, friction, coriolis
        )
    return jnp.stack([height, eastward, northward], axis=1)


def class_tables(accuracy_levels):
    onehot = (accuracy_levels[:, None] == jnp.arange(3)[None, :]).astype(jnp.float32)
    counts = jnp.sum(onehot, axis=0)
    coefs = jnp.stack(
        [
            1.0 / (counts[0] - 1.0),
            -control_weight / (counts[1] - 1.0),
            control_weight / (counts[2] - 1.0),
        ]
    )
    member_weight = jnp.sum(onehot * coefs[None, :], axis=1)
    return (onehot, counts, member_weight)


def remove_means(data, onehot, counts):
    means = jnp.dot(onehot.T, data, precision=exact) / counts[:, None]
    return data - jnp.dot(onehot, means, precision=exact)


def spd_solve(factor, rhs):
    inner = lax.linalg.triangular_solve(factor, rhs, left_side=True, lower=True)
    return lax.linalg.triangular_solve(factor, inner, left_side=True, lower=True, transpose_a=True)


def gauss_jordan_steps(a):
    n = a.shape[0]
    lane = lax.broadcasted_iota(jnp.int32, a.shape, 1)
    row_id = lax.broadcasted_iota(jnp.int32, (n, 1), 0)
    if n <= 64:
        for k in range(n):
            pivot_row = a[k : k + 1, :] * (1.0 / a[k : k + 1, k : k + 1])
            column = a[:, k : k + 1] - (row_id == k).astype(jnp.float32)
            a = a - column * pivot_row
        return a

    def step(k, a):
        pivot_row = jnp.sum(jnp.where(row_id == k, a, 0.0), axis=0, keepdims=True)
        column = jnp.sum(jnp.where(lane == k, a, 0.0), axis=1, keepdims=True)
        pivot = jnp.sum(jnp.where(lane[0:1] == k, pivot_row, 0.0), axis=1, keepdims=True)
        pivot_row = pivot_row / pivot
        column = column - (row_id == k).astype(jnp.float32)
        return a - column * pivot_row

    return lax.fori_loop(0, n, step, a)

def contract(a, b, dims):
    return lax.dot_general(
        a, b, (dims, ((), ())), precision=exact, preferred_element_type=jnp.float32
    )


def analysis_kernel(x_ref, ob_ref, fid_col_ref, fid_row_ref, value_ref, var_ref, noise_ref, o_ref):
    per_device = fid_col_ref.shape[1]
    width = x_ref.shape[2] // per_device
    x = jnp.concatenate([x_ref[:, 0, i * width : (i + 1) * width] for i in range(per_device)], axis=0)
    m = x.shape[0]
    ob = ob_ref[...]
    fid_col = jnp.concatenate([fid_col_ref[:, i : i + 1] for i in range(per_device)], axis=0)
    fid_row = jnp.concatenate([fid_row_ref[i : i + 1, :] for i in range(per_device)], axis=1)
    variance = var_ref[...]
    masks = [(fid_col == c).astype(jnp.float32) for c in range(3)]
    masks_row = [(fid_row == c).astype(jnp.float32) for c in range(3)]
    counts = [jnp.sum(mask, axis=0, keepdims=True) for mask in masks]

    def remove_means(data):
        centred = data
        for mask, count in zip(masks, counts):
            centred = centred - mask * (jnp.sum(mask * data, axis=0, keepdims=True) / count)
        return centred

    spread = remove_means(x)
    obs_spread = remove_means(ob)
    weight = (
        masks[0] * (1.0 / (counts[0] - 1.0))
        + masks[1] * (-control_weight / (counts[1] - 1.0))
        + masks[2] * (control_weight / (counts[2] - 1.0))
    )
    scale_col = jnp.sqrt(masks[0] / (counts[0] - 1.0))
    count_row = jnp.sum(masks_row[0], axis=1, keepdims=True)
    scale_row = jnp.sqrt(masks_row[0] / (count_row - 1.0))
    weighted = obs_spread / variance
    inner = contract(weighted, obs_spread, ((1,), (1,)))
    direct = (
        jnp.sum(weighted * value_ref[...], axis=1, keepdims=True)
        + contract(weighted * jnp.sqrt(variance), noise_ref[...], ((1,), (0,)))
        - contract(weighted, ob, ((1,), (1,)))
    )
    row_id = lax.broadcasted_iota(jnp.int32, (m, m), 0)
    col_id = lax.broadcasted_iota(jnp.int32, (m, m), 1)
    system = (row_id == col_id).astype(jnp.float32) + scale_col * inner * scale_row
    augmented = jnp.concatenate([system, scale_col * direct], axis=1)
    solved = gauss_jordan_steps(augmented)[:, m:]
    projected = direct - contract(inner, scale_col * solved, ((1,), (0,)))
    mixing = projected * weight
    result = x + contract(mixing, spread, ((0,), (0,)))
    sources = x_ref.shape[0]
    for i in range(per_device):
        o_ref[:, 0, i * width : (i + 1) * width] = result[i * sources : (i + 1) * sources]


def analysis(rows, observed, fidelity, value, variance, noise):
    sources = rows.shape[0]
    vmem = pl.BlockSpec(memory_space=pltpu.VMEM)
    return pl.pallas_call(
        analysis_kernel,
        out_shape=jax.ShapeDtypeStruct(rows.shape, jnp.float32),
        in_specs=[vmem] * 7,
        out_specs=vmem,
        compiler_params=pltpu.CompilerParams(vmem_limit_bytes=48 * 1024 * 1024),
    )(
        rows,
        observed,
        fidelity.reshape(sources, -1),
        fidelity.reshape(sources, -1).T,
        value.reshape(1, -1),
        variance.reshape(1, -1),
        noise,
    )


def shifted(field, offset, axis):
    size = field.shape[axis]
    rolled = pltpu.roll(field, (-offset) % size, axis)
    place = lax.broadcasted_iota(jnp.int32, field.shape, axis) + offset
    return jnp.where((place >= 0) & (place < size), rolled, 0.0)


def kernel_neighbours(field):
    return (shifted(field, 1, 1), shifted(field, -1, 1), shifted(field, 1, 0), shifted(field, -1, 0))


def kernel_east(field):
    ahead, behind, upper, lower = kernel_neighbours(field)
    return 0.5 * (ahead - behind)


def kernel_north(field):
    ahead, behind, upper, lower = kernel_neighbours(field)
    return 0.5 * (upper - lower)


def kernel_laplace(field):
    ahead, behind, upper, lower = kernel_neighbours(field)
    return ahead + behind + upper + lower - 4.0 * field


def forecast_kernel(fid_ref, x_ref, o_ref):
    members, _, lat_rows, lon = x_ref.shape
    first = lax.axis_index("band") * members
    row = lax.broadcasted_iota(jnp.int32, (lat_rows, 1), 0).astype(jnp.float32)
    coriolis = 0.1 + 0.2 * (row + 0.5) / lat_rows
    for member in range(members):
        level = fid_ref[first + member]
        nonlinear = jnp.where(level == 0, 1.0, 0.0).astype(jnp.float32)
        friction = jnp.where(level == 0, 0.0, slow_friction).astype(jnp.float32)
        height, eastward, northward = x_ref[member, 0], x_ref[member, 1], x_ref[member, 2]
        for step in range(PREDICTION_COUNT):
            depth = 1.0 + nonlinear * height
            height_new = (
                height
                - time_step * (kernel_east(depth * eastward) + kernel_north(depth * northward))
                + time_step * viscous * kernel_laplace(height)
            )
            east_new = eastward + time_step * (
                -nonlinear * (eastward * kernel_east(eastward) + northward * kernel_north(eastward))
                + coriolis * northward
                - kernel_east(height_new)
                + viscous * kernel_laplace(eastward)
                - friction * eastward
            )
            north_new = northward + time_step * (
                -nonlinear * (eastward * kernel_east(northward) + northward * kernel_north(northward))
                - coriolis * eastward
                - kernel_north(height_new)
                + viscous * kernel_laplace(northward)
                - friction * northward
            )
            height, eastward, northward = height_new, east_new, north_new
        for component, field in enumerate((height, eastward, northward)):
            o_ref[:, 0, pl.ds((member * 3 + component) * lon, lon)] = field


def forecast(initial, levels):
    members, components, lat_rows, lon = initial.shape
    return pl.pallas_call(
        forecast_kernel,
        out_shape=jax.ShapeDtypeStruct((lat_rows, 1, members * components * lon), jnp.float32),
        in_specs=[
            pl.BlockSpec(memory_space=pltpu.SMEM),
            pl.BlockSpec(memory_space=pltpu.VMEM),
        ],
        out_specs=pl.BlockSpec(memory_space=pltpu.VMEM),
    )(levels, initial)


def unpack_kernel(x_ref, o_ref):
    members, components, _, lon = o_ref.shape
    for member in range(members):
        for component in range(components):
            o_ref[member, component] = x_ref[:, 0, pl.ds((member * components + component) * lon, lon)]


def unpack(rows, shape):
    return pl.pallas_call(
        unpack_kernel,
        out_shape=jax.ShapeDtypeStruct(shape, jnp.float32),
        in_specs=[pl.BlockSpec(memory_space=pltpu.VMEM)],
        out_specs=pl.BlockSpec(memory_space=pltpu.VMEM),
    )(rows)


def shards(initial_height_velocity, member_fidelity, obs_cell, obs_value, obs_var, obs_noise):
    per_device, components, lat_rows, lon = initial_height_velocity.shape
    sources = lax.axis_size("band")
    rows = forecast(initial_height_velocity, member_fidelity)
    rows = lax.all_to_all(rows, "band", 0, 0, tiled=True)
    up = [(i, i + 1) for i in range(sources - 1)]
    down = [(j, i) for i, j in up]
    below = lax.ppermute(rows, "band", up)
    above = lax.ppermute(rows, "band", down)
    block = jnp.concatenate([below, rows, above], axis=1).reshape(sources, 3, per_device, components, lon)
    block = jnp.transpose(block, (2, 0, 3, 1, 4)).reshape(sources * per_device, -1)
    observed = jnp.take(block, obs_cell[0], axis=1)
    noise = obs_noise[0].reshape(-1, sources, per_device)
    noise = jnp.transpose(noise, (0, 2, 1)).reshape(-1, sources * per_device)
    result = analysis(rows, observed, member_fidelity, obs_value[0], obs_var[0], noise)
    result = lax.all_to_all(result, "band", 0, 0, tiled=True)
    return unpack(result, initial_height_velocity.shape)


def solution(mesh):
    in_specs = (
        P(("groups", "band"), None, None, None),
        P("groups"),
        P(("groups", "band"), None),
        P(("groups", "band"), None),
        P(("groups", "band"), None),
        P(("groups", "band"), None, None),
    )
    out_specs = P(("groups", "band"), None, None, None)
    return jax.shard_map(shards, mesh=mesh, in_specs=in_specs, out_specs=out_specs, check_vma=False)
```

```python
import jax
import jax.numpy as jnp
from jax import lax
from jax.sharding import PartitionSpec as P
from jax.experimental import pallas as pl
from jax.experimental.pallas import tpu as pltpu

PREDICTION_COUNT = 4


exact = lax.Precision.HIGHEST
time_step = 0.25
viscous = 0.05
slow_friction = 0.2
control_weight = 0.5


def extended(shard, sides, width):
    for axis, dim in sides:
        devices, length = (lax.axis_size(axis), shard.shape[dim])
        up = [(i, (i + 1) % devices) for i in range(devices - 1)]
        down = [(j, i) for i, j in up]
        last = lax.slice_in_dim(shard, length - width, length, axis=dim)
        leading = lax.slice_in_dim(shard, 0, width, axis=dim)
        before = lax.ppermute(last, axis, up)
        after = lax.ppermute(leading, axis, down)
        shard = jnp.concatenate([before, shard, after], axis=dim)
    return shard


def neighbours(field):
    lon_pad = jnp.pad(field, [(0, 0)] * (field.ndim - 1) + [(1, 1)])
    lat_pad = jnp.pad(field, [(0, 0)] * (field.ndim - 2) + [(1, 1), (0, 0)])
    return (lon_pad[..., 2:], lon_pad[..., :-2], lat_pad[..., 2:, :], lat_pad[..., :-2, :])


def east_slope(field):
    ahead, behind, upper, lower = neighbours(field)
    return 0.5 * (ahead - behind)


def north_slope(field):
    ahead, behind, upper, lower = neighbours(field)
    return 0.5 * (upper - lower)


def laplace(field):
    ahead, behind, upper, lower = neighbours(field)
    return ahead + behind + upper + lower - 4.0 * field


def advance(height, eastward, northward, nonlinear, friction, coriolis):
    depth = 1.0 + nonlinear * height
    height_new = (
        height
        - time_step * (east_slope(depth * eastward) + north_slope(depth * northward))
        + time_step * viscous * laplace(height)
    )
    east_new = eastward + time_step * (
        -nonlinear * (eastward * east_slope(eastward) + northward * north_slope(eastward))
        + coriolis * northward
        - east_slope(height_new)
        + viscous * laplace(eastward)
        - friction * eastward
    )
    north_new = northward + time_step * (
        -nonlinear * (eastward * east_slope(northward) + northward * north_slope(northward))
        - coriolis * eastward
        - north_slope(height_new)
        + viscous * laplace(northward)
        - friction * northward
    )
    return (height_new, east_new, north_new)


def begin_prediction(marine_condition, accuracy_levels, realization_count):
    nonlinear = (accuracy_levels == 0).astype(jnp.float32)[:, None, None]
    friction = jnp.where(accuracy_levels == 0, 0.0, slow_friction).astype(jnp.float32)[
        :, None, None
    ]
    lat_rows = marine_condition.shape[2]
    coriolis = (0.1 + 0.2 * (jnp.arange(lat_rows).astype(jnp.float32) + 0.5) / lat_rows)[:, None]
    height, eastward, northward = (
        marine_condition[:, 0],
        marine_condition[:, 1],
        marine_condition[:, 2],
    )
    for step in range(realization_count):
        height, eastward, northward = advance(
            height, eastward, northward, nonlinear, friction, coriolis
        )
    return jnp.stack([height, eastward, northward], axis=1)


def class_tables(accuracy_levels):
    onehot = (accuracy_levels[:, None] == jnp.arange(3)[None, :]).astype(jnp.float32)
    counts = jnp.sum(onehot, axis=0)
    coefs = jnp.stack(
        [
            1.0 / (counts[0] - 1.0),
            -control_weight / (counts[1] - 1.0),
            control_weight / (counts[2] - 1.0),
        ]
    )
    member_weight = jnp.sum(onehot * coefs[None, :], axis=1)
    return (onehot, counts, member_weight)


def remove_means(data, onehot, counts):
    means = jnp.dot(onehot.T, data, precision=exact) / counts[:, None]
    return data - jnp.dot(onehot, means, precision=exact)


def spd_solve(factor, rhs):
    inner = lax.linalg.triangular_solve(factor, rhs, left_side=True, lower=True)
    return lax.linalg.triangular_solve(factor, inner, left_side=True, lower=True, transpose_a=True)


def gauss_jordan_steps(a):
    n = a.shape[0]
    lane = lax.broadcasted_iota(jnp.int32, a.shape, 1)
    row_id = lax.broadcasted_iota(jnp.int32, (n, 1), 0)
    if n <= 64:
        for k in range(n):
            pivot_row = a[k : k + 1, :] * (1.0 / a[k : k + 1, k : k + 1])
            column = a[:, k : k + 1] - (row_id == k).astype(jnp.float32)
            a = a - column * pivot_row
        return a

    def step(k, a):
        pivot_row = jnp.sum(jnp.where(row_id == k, a, 0.0), axis=0, keepdims=True)
        column = jnp.sum(jnp.where(lane == k, a, 0.0), axis=1, keepdims=True)
        pivot = jnp.sum(jnp.where(lane[0:1] == k, pivot_row, 0.0), axis=1, keepdims=True)
        pivot_row = pivot_row / pivot
        column = column - (row_id == k).astype(jnp.float32)
        return a - column * pivot_row

    return lax.fori_loop(0, n, step, a)

def contract(a, b, dims):
    return lax.dot_general(
        a, b, (dims, ((), ())), precision=exact, preferred_element_type=jnp.float32
    )


def analysis_kernel(
    cell_ref, below_ref, x_ref, above_ref, fid_col_ref, fid_row_ref, value_ref, var_ref, noise_ref,
    o_ref, cells_ref, picked_ref,
):
    per_device = fid_col_ref.shape[1]
    width = x_ref.shape[2] // per_device
    def members_of(ref):
        return jnp.concatenate([ref[:, 0, i * width : (i + 1) * width] for i in range(per_device)], axis=0)
    x = members_of(x_ref)
    m = x.shape[0]
    components = 3
    lon = width // components
    for offset, ref in enumerate((below_ref, x_ref, above_ref)):
        block = x if offset == 1 else members_of(ref)
        block = block.T
        for component in range(components):
            cells_ref[pl.ds((component * 3 + offset) * lon, lon), :] = block[component * lon : (component + 1) * lon]

    def pick(o, carry):
        picked_ref[pl.ds(o, 1), :] = cells_ref[pl.ds(cell_ref[o], 1), :]
        return carry

    lax.fori_loop(0, picked_ref.shape[0], pick, 0, unroll=8)
    ob = picked_ref[...].T
    fid_col = jnp.concatenate([fid_col_ref[:, i : i + 1] for i in range(per_device)], axis=0)
    fid_row = jnp.concatenate([fid_row_ref[i : i + 1, :] for i in range(per_device)], axis=1)
    variance = var_ref[...]
    masks = [(fid_col == c).astype(jnp.float32) for c in range(3)]
    masks_row = [(fid_row == c).astype(jnp.float32) for c in range(3)]
    counts = [jnp.sum(mask, axis=0, keepdims=True) for mask in masks]

    def remove_means(data):
        centred = data
        for mask, count in zip(masks, counts):
            centred = centred - mask * (jnp.sum(mask * data, axis=0, keepdims=True) / count)
        return centred

    spread = remove_means(x)
    obs_spread = remove_means(ob)
    weight = (
        masks[0] * (1.0 / (counts[0] - 1.0))
        + masks[1] * (-control_weight / (counts[1] - 1.0))
        + masks[2] * (control_weight / (counts[2] - 1.0))
    )
    scale_col = jnp.sqrt(masks[0] / (counts[0] - 1.0))
    count_row = jnp.sum(masks_row[0], axis=1, keepdims=True)
    scale_row = jnp.sqrt(masks_row[0] / (count_row - 1.0))
    weighted = obs_spread / variance
    inner = contract(weighted, obs_spread, ((1,), (1,)))
    direct = (
        jnp.sum(weighted * value_ref[...], axis=1, keepdims=True)
        + contract(weighted * jnp.sqrt(variance), noise_ref[...], ((1,), (0,)))
        - contract(weighted, ob, ((1,), (1,)))
    )
    row_id = lax.broadcasted_iota(jnp.int32, (m, m), 0)
    col_id = lax.broadcasted_iota(jnp.int32, (m, m), 1)
    system = (row_id == col_id).astype(jnp.float32) + scale_col * inner * scale_row
    augmented = jnp.concatenate([system, scale_col * direct], axis=1)
    solved = gauss_jordan_steps(augmented)[:, m:]
    projected = direct - contract(inner, scale_col * solved, ((1,), (0,)))
    mixing = projected * weight
    result = x + contract(mixing, spread, ((0,), (0,)))
    sources = x_ref.shape[0]
    for i in range(per_device):
        o_ref[:, 0, i * width : (i + 1) * width] = result[i * sources : (i + 1) * sources]


def analysis(cells, below, rows, above, fidelity, value, variance, noise):
    sources = rows.shape[0]
    members = fidelity.shape[0]
    vmem = pl.BlockSpec(memory_space=pltpu.VMEM)
    return pl.pallas_call(
        analysis_kernel,
        out_shape=jax.ShapeDtypeStruct(rows.shape, jnp.float32),
        in_specs=[pl.BlockSpec(memory_space=pltpu.SMEM)] + [vmem] * 8,
        out_specs=vmem,
        scratch_shapes=[
            pltpu.VMEM((3 * rows.shape[2] // (members // sources), members), jnp.float32),
            pltpu.VMEM((cells.shape[0], members), jnp.float32),
        ],
        compiler_params=pltpu.CompilerParams(vmem_limit_bytes=48 * 1024 * 1024),
    )(
        cells,
        below,
        rows,
        above,
        fidelity.reshape(sources, -1),
        fidelity.reshape(sources, -1).T,
        value.reshape(1, -1),
        variance.reshape(1, -1),
        noise,
    )


def shifted(field, offset, axis):
    size = field.shape[axis]
    rolled = pltpu.roll(field, (-offset) % size, axis)
    place = lax.broadcasted_iota(jnp.int32, field.shape, axis) + offset
    return jnp.where((place >= 0) & (place < size), rolled, 0.0)


def kernel_neighbours(field):
    return (shifted(field, 1, 1), shifted(field, -1, 1), shifted(field, 1, 0), shifted(field, -1, 0))


def kernel_east(field):
    ahead, behind, upper, lower = kernel_neighbours(field)
    return 0.5 * (ahead - behind)


def kernel_north(field):
    ahead, behind, upper, lower = kernel_neighbours(field)
    return 0.5 * (upper - lower)


def kernel_laplace(field):
    ahead, behind, upper, lower = kernel_neighbours(field)
    return ahead + behind + upper + lower - 4.0 * field


def forecast_kernel(fid_ref, x_ref, o_ref):
    members, _, lat_rows, lon = x_ref.shape
    first = lax.axis_index("band") * members
    row = lax.broadcasted_iota(jnp.int32, (lat_rows, 1), 0).astype(jnp.float32)
    coriolis = 0.1 + 0.2 * (row + 0.5) / lat_rows
    for member in range(members):
        level = fid_ref[first + member]
        nonlinear = jnp.where(level == 0, 1.0, 0.0).astype(jnp.float32)
        friction = jnp.where(level == 0, 0.0, slow_friction).astype(jnp.float32)
        height, eastward, northward = x_ref[member, 0], x_ref[member, 1], x_ref[member, 2]
        for step in range(PREDICTION_COUNT):
            depth = 1.0 + nonlinear * height
            height_new = (
                height
                - time_step * (kernel_east(depth * eastward) + kernel_north(depth * northward))
                + time_step * viscous * kernel_laplace(height)
            )
            east_new = eastward + time_step * (
                -nonlinear * (eastward * kernel_east(eastward) + northward * kernel_north(eastward))
                + coriolis * northward
                - kernel_east(height_new)
                + viscous * kernel_laplace(eastward)
                - friction * eastward
            )
            north_new = northward + time_step * (
                -nonlinear * (eastward * kernel_east(northward) + northward * kernel_north(northward))
                - coriolis * eastward
                - kernel_north(height_new)
                + viscous * kernel_laplace(northward)
                - friction * northward
            )
            height, eastward, northward = height_new, east_new, north_new
        for component, field in enumerate((height, eastward, northward)):
            o_ref[:, 0, pl.ds((member * 3 + component) * lon, lon)] = field


def forecast(initial, levels):
    members, components, lat_rows, lon = initial.shape
    return pl.pallas_call(
        forecast_kernel,
        out_shape=jax.ShapeDtypeStruct((lat_rows, 1, members * components * lon), jnp.float32),
        in_specs=[
            pl.BlockSpec(memory_space=pltpu.SMEM),
            pl.BlockSpec(memory_space=pltpu.VMEM),
        ],
        out_specs=pl.BlockSpec(memory_space=pltpu.VMEM),
    )(levels, initial)


def shards(initial_height_velocity, member_fidelity, obs_cell, obs_value, obs_var, obs_noise):
    per_device, components, lat_rows, lon = initial_height_velocity.shape
    sources = lax.axis_size("band")
    rows = forecast(initial_height_velocity, member_fidelity)
    rows = lax.all_to_all(rows, "band", 0, 0, tiled=True)
    up = [(i, i + 1) for i in range(sources - 1)]
    down = [(j, i) for i, j in up]
    below = lax.ppermute(rows, "band", up)
    above = lax.ppermute(rows, "band", down)
    noise = obs_noise[0].reshape(-1, sources, per_device)
    noise = jnp.transpose(noise, (0, 2, 1)).reshape(-1, sources * per_device)
    result = analysis(obs_cell[0], below, rows, above, member_fidelity, obs_value[0], obs_var[0], noise)
    result = lax.all_to_all(result, "band", 0, 0, tiled=True)
    result = result.reshape(lat_rows, per_device, components, lon)
    return jnp.transpose(result, (1, 2, 0, 3))


def solution(mesh):
    in_specs = (
        P(("groups", "band"), None, None, None),
        P("groups"),
        P(("groups", "band"), None),
        P(("groups", "band"), None),
        P(("groups", "band"), None),
        P(("groups", "band"), None, None),
    )
    out_specs = P(("groups", "band"), None, None, None)
    return jax.shard_map(shards, mesh=mesh, in_specs=in_specs, out_specs=out_specs, check_vma=False)
```

```python
import jax
import jax.numpy as jnp
from jax import lax
from jax.sharding import PartitionSpec as P
from jax.experimental import pallas as pl
from jax.experimental.pallas import tpu as pltpu

PREDICTION_COUNT = 4


exact = lax.Precision.HIGHEST
time_step = 0.25
viscous = 0.05
slow_friction = 0.2
control_weight = 0.5


def extended(shard, sides, width):
    for axis, dim in sides:
        devices, length = (lax.axis_size(axis), shard.shape[dim])
        up = [(i, (i + 1) % devices) for i in range(devices - 1)]
        down = [(j, i) for i, j in up]
        last = lax.slice_in_dim(shard, length - width, length, axis=dim)
        leading = lax.slice_in_dim(shard, 0, width, axis=dim)
        before = lax.ppermute(last, axis, up)
        after = lax.ppermute(leading, axis, down)
        shard = jnp.concatenate([before, shard, after], axis=dim)
    return shard


def neighbours(field):
    lon_pad = jnp.pad(field, [(0, 0)] * (field.ndim - 1) + [(1, 1)])
    lat_pad = jnp.pad(field, [(0, 0)] * (field.ndim - 2) + [(1, 1), (0, 0)])
    return (lon_pad[..., 2:], lon_pad[..., :-2], lat_pad[..., 2:, :], lat_pad[..., :-2, :])


def east_slope(field):
    ahead, behind, upper, lower = neighbours(field)
    return 0.5 * (ahead - behind)


def north_slope(field):
    ahead, behind, upper, lower = neighbours(field)
    return 0.5 * (upper - lower)


def laplace(field):
    ahead, behind, upper, lower = neighbours(field)
    return ahead + behind + upper + lower - 4.0 * field


def advance(height, eastward, northward, nonlinear, friction, coriolis):
    depth = 1.0 + nonlinear * height
    height_new = (
        height
        - time_step * (east_slope(depth * eastward) + north_slope(depth * northward))
        + time_step * viscous * laplace(height)
    )
    east_new = eastward + time_step * (
        -nonlinear * (eastward * east_slope(eastward) + northward * north_slope(eastward))
        + coriolis * northward
        - east_slope(height_new)
        + viscous * laplace(eastward)
        - friction * eastward
    )
    north_new = northward + time_step * (
        -nonlinear * (eastward * east_slope(northward) + northward * north_slope(northward))
        - coriolis * eastward
        - north_slope(height_new)
        + viscous * laplace(northward)
        - friction * northward
    )
    return (height_new, east_new, north_new)


def begin_prediction(marine_condition, accuracy_levels, realization_count):
    nonlinear = (accuracy_levels == 0).astype(jnp.float32)[:, None, None]
    friction = jnp.where(accuracy_levels == 0, 0.0, slow_friction).astype(jnp.float32)[
        :, None, None
    ]
    lat_rows = marine_condition.shape[2]
    coriolis = (0.1 + 0.2 * (jnp.arange(lat_rows).astype(jnp.float32) + 0.5) / lat_rows)[:, None]
    height, eastward, northward = (
        marine_condition[:, 0],
        marine_condition[:, 1],
        marine_condition[:, 2],
    )
    for step in range(realization_count):
        height, eastward, northward = advance(
            height, eastward, northward, nonlinear, friction, coriolis
        )
    return jnp.stack([height, eastward, northward], axis=1)


def class_tables(accuracy_levels):
    onehot = (accuracy_levels[:, None] == jnp.arange(3)[None, :]).astype(jnp.float32)
    counts = jnp.sum(onehot, axis=0)
    coefs = jnp.stack(
        [
            1.0 / (counts[0] - 1.0),
            -control_weight / (counts[1] - 1.0),
            control_weight / (counts[2] - 1.0),
        ]
    )
    member_weight = jnp.sum(onehot * coefs[None, :], axis=1)
    return (onehot, counts, member_weight)


def remove_means(data, onehot, counts):
    means = jnp.dot(onehot.T, data, precision=exact) / counts[:, None]
    return data - jnp.dot(onehot, means, precision=exact)


def spd_solve(factor, rhs):
    inner = lax.linalg.triangular_solve(factor, rhs, left_side=True, lower=True)
    return lax.linalg.triangular_solve(factor, inner, left_side=True, lower=True, transpose_a=True)


def gauss_jordan_steps(a):
    n = a.shape[0]
    lane = lax.broadcasted_iota(jnp.int32, a.shape, 1)
    row_id = lax.broadcasted_iota(jnp.int32, (n, 1), 0)
    if n <= 64:
        for k in range(n):
            pivot_row = a[k : k + 1, :] * (1.0 / a[k : k + 1, k : k + 1])
            column = a[:, k : k + 1] - (row_id == k).astype(jnp.float32)
            a = a - column * pivot_row
        return a

    def step(k, a):
        pivot_row = jnp.sum(jnp.where(row_id == k, a, 0.0), axis=0, keepdims=True)
        column = jnp.sum(jnp.where(lane == k, a, 0.0), axis=1, keepdims=True)
        pivot = jnp.sum(jnp.where(lane[0:1] == k, pivot_row, 0.0), axis=1, keepdims=True)
        pivot_row = pivot_row / pivot
        column = column - (row_id == k).astype(jnp.float32)
        return a - column * pivot_row

    return lax.fori_loop(0, n, step, a)

def contract(a, b, dims):
    return lax.dot_general(
        a, b, (dims, ((), ())), precision=exact, preferred_element_type=jnp.float32
    )


def analysis_kernel(
    cell_ref, below_ref, x_ref, above_ref, fid_col_ref, fid_row_ref, value_ref, var_ref, noise_ref,
    o_ref, cells_ref, picked_ref,
):
    per_device = fid_col_ref.shape[1]
    width = x_ref.shape[2] // per_device
    def members_of(ref):
        return jnp.concatenate([ref[:, 0, i * width : (i + 1) * width] for i in range(per_device)], axis=0)
    x = members_of(x_ref)
    m = x.shape[0]
    components = 3
    lon = width // components
    for offset, ref in enumerate((below_ref, x_ref, above_ref)):
        block = x if offset == 1 else members_of(ref)
        block = block.T
        for component in range(components):
            cells_ref[pl.ds((component * 3 + offset) * lon, lon), :] = block[component * lon : (component + 1) * lon]

    def pick(o, carry):
        picked_ref[pl.ds(o, 1), :] = cells_ref[pl.ds(cell_ref[o], 1), :]
        return carry

    lax.fori_loop(0, picked_ref.shape[0], pick, 0, unroll=picked_ref.shape[0] <= 512 or 8)
    ob = picked_ref[...].T
    fid_col = jnp.concatenate([fid_col_ref[:, i : i + 1] for i in range(per_device)], axis=0)
    fid_row = jnp.concatenate([fid_row_ref[i : i + 1, :] for i in range(per_device)], axis=1)
    variance = var_ref[...]
    masks = [(fid_col == c).astype(jnp.float32) for c in range(3)]
    masks_row = [(fid_row == c).astype(jnp.float32) for c in range(3)]
    counts = [jnp.sum(mask, axis=0, keepdims=True) for mask in masks]

    def remove_means(data):
        centred = data
        for mask, count in zip(masks, counts):
            centred = centred - mask * (jnp.sum(mask * data, axis=0, keepdims=True) / count)
        return centred

    spread = remove_means(x)
    obs_spread = remove_means(ob)
    weight = (
        masks[0] * (1.0 / (counts[0] - 1.0))
        + masks[1] * (-control_weight / (counts[1] - 1.0))
        + masks[2] * (control_weight / (counts[2] - 1.0))
    )
    scale_col = jnp.sqrt(masks[0] / (counts[0] - 1.0))
    count_row = jnp.sum(masks_row[0], axis=1, keepdims=True)
    scale_row = jnp.sqrt(masks_row[0] / (count_row - 1.0))
    weighted = obs_spread / variance
    inner = contract(weighted, obs_spread, ((1,), (1,)))
    direct = (
        jnp.sum(weighted * value_ref[...], axis=1, keepdims=True)
        + contract(weighted * jnp.sqrt(variance), noise_ref[...], ((1,), (0,)))
        - contract(weighted, ob, ((1,), (1,)))
    )
    row_id = lax.broadcasted_iota(jnp.int32, (m, m), 0)
    col_id = lax.broadcasted_iota(jnp.int32, (m, m), 1)
    system = (row_id == col_id).astype(jnp.float32) + scale_col * inner * scale_row
    augmented = jnp.concatenate([system, scale_col * direct], axis=1)
    solved = gauss_jordan_steps(augmented)[:, m:]
    projected = direct - contract(inner, scale_col * solved, ((1,), (0,)))
    mixing = projected * weight
    result = x + contract(mixing, spread, ((0,), (0,)))
    sources = x_ref.shape[0]
    for i in range(per_device):
        o_ref[:, 0, i * width : (i + 1) * width] = result[i * sources : (i + 1) * sources]


def analysis(cells, below, rows, above, fidelity, value, variance, noise):
    sources = rows.shape[0]
    members = fidelity.shape[0]
    vmem = pl.BlockSpec(memory_space=pltpu.VMEM)
    return pl.pallas_call(
        analysis_kernel,
        out_shape=jax.ShapeDtypeStruct(rows.shape, jnp.float32),
        in_specs=[pl.BlockSpec(memory_space=pltpu.SMEM)] + [vmem] * 8,
        out_specs=vmem,
        scratch_shapes=[
            pltpu.VMEM((3 * rows.shape[2] // (members // sources), members), jnp.float32),
            pltpu.VMEM((cells.shape[0], members), jnp.float32),
        ],
        compiler_params=pltpu.CompilerParams(vmem_limit_bytes=48 * 1024 * 1024),
    )(
        cells,
        below,
        rows,
        above,
        fidelity.reshape(sources, -1),
        fidelity.reshape(sources, -1).T,
        value.reshape(1, -1),
        variance.reshape(1, -1),
        noise,
    )


def shifted(field, offset, axis):
    size = field.shape[axis]
    rolled = pltpu.roll(field, (-offset) % size, axis)
    place = lax.broadcasted_iota(jnp.int32, field.shape, axis) + offset
    return jnp.where((place >= 0) & (place < size), rolled, 0.0)


def kernel_neighbours(field):
    return (shifted(field, 1, 1), shifted(field, -1, 1), shifted(field, 1, 0), shifted(field, -1, 0))


def kernel_east(field):
    ahead, behind, upper, lower = kernel_neighbours(field)
    return 0.5 * (ahead - behind)


def kernel_north(field):
    ahead, behind, upper, lower = kernel_neighbours(field)
    return 0.5 * (upper - lower)


def kernel_laplace(field):
    ahead, behind, upper, lower = kernel_neighbours(field)
    return ahead + behind + upper + lower - 4.0 * field


def forecast_kernel(fid_ref, x_ref, o_ref):
    members, _, lat_rows, lon = x_ref.shape
    first = lax.axis_index("band") * members
    row = lax.broadcasted_iota(jnp.int32, (lat_rows, 1), 0).astype(jnp.float32)
    coriolis = 0.1 + 0.2 * (row + 0.5) / lat_rows
    for member in range(members):
        level = fid_ref[first + member]
        nonlinear = jnp.where(level == 0, 1.0, 0.0).astype(jnp.float32)
        friction = jnp.where(level == 0, 0.0, slow_friction).astype(jnp.float32)
        height, eastward, northward = x_ref[member, 0], x_ref[member, 1], x_ref[member, 2]
        for step in range(PREDICTION_COUNT):
            depth = 1.0 + nonlinear * height
            height_new = (
                height
                - time_step * (kernel_east(depth * eastward) + kernel_north(depth * northward))
                + time_step * viscous * kernel_laplace(height)
            )
            east_new = eastward + time_step * (
                -nonlinear * (eastward * kernel_east(eastward) + northward * kernel_north(eastward))
                + coriolis * northward
                - kernel_east(height_new)
                + viscous * kernel_laplace(eastward)
                - friction * eastward
            )
            north_new = northward + time_step * (
                -nonlinear * (eastward * kernel_east(northward) + northward * kernel_north(northward))
                - coriolis * eastward
                - kernel_north(height_new)
                + viscous * kernel_laplace(northward)
                - friction * northward
            )
            height, eastward, northward = height_new, east_new, north_new
        for component, field in enumerate((height, eastward, northward)):
            o_ref[:, 0, pl.ds((member * 3 + component) * lon, lon)] = field


def forecast(initial, levels):
    members, components, lat_rows, lon = initial.shape
    return pl.pallas_call(
        forecast_kernel,
        out_shape=jax.ShapeDtypeStruct((lat_rows, 1, members * components * lon), jnp.float32),
        in_specs=[
            pl.BlockSpec(memory_space=pltpu.SMEM),
            pl.BlockSpec(memory_space=pltpu.VMEM),
        ],
        out_specs=pl.BlockSpec(memory_space=pltpu.VMEM),
    )(levels, initial)


def shards(initial_height_velocity, member_fidelity, obs_cell, obs_value, obs_var, obs_noise):
    per_device, components, lat_rows, lon = initial_height_velocity.shape
    sources = lax.axis_size("band")
    rows = forecast(initial_height_velocity, member_fidelity)
    rows = lax.all_to_all(rows, "band", 0, 0, tiled=True)
    up = [(i, i + 1) for i in range(sources - 1)]
    down = [(j, i) for i, j in up]
    below = lax.ppermute(rows, "band", up)
    above = lax.ppermute(rows, "band", down)
    noise = obs_noise[0].reshape(-1, sources, per_device)
    noise = jnp.transpose(noise, (0, 2, 1)).reshape(-1, sources * per_device)
    result = analysis(obs_cell[0], below, rows, above, member_fidelity, obs_value[0], obs_var[0], noise)
    result = lax.all_to_all(result, "band", 0, 0, tiled=True)
    result = result.reshape(lat_rows, per_device, components, lon)
    return jnp.transpose(result, (1, 2, 0, 3))


def solution(mesh):
    in_specs = (
        P(("groups", "band"), None, None, None),
        P("groups"),
        P(("groups", "band"), None),
        P(("groups", "band"), None),
        P(("groups", "band"), None),
        P(("groups", "band"), None, None),
    )
    out_specs = P(("groups", "band"), None, None, None)
    return jax.shard_map(shards, mesh=mesh, in_specs=in_specs, out_specs=out_specs, check_vma=False)
```

```python
import jax
import jax.numpy as jnp
from jax import lax
from jax.sharding import PartitionSpec as P
from jax.experimental import pallas as pl
from jax.experimental.pallas import tpu as pltpu

PREDICTION_COUNT = 4


exact = lax.Precision.HIGHEST
time_step = 0.25
viscous = 0.05
slow_friction = 0.2
control_weight = 0.5


def extended(shard, sides, width):
    for axis, dim in sides:
        devices, length = (lax.axis_size(axis), shard.shape[dim])
        up = [(i, (i + 1) % devices) for i in range(devices - 1)]
        down = [(j, i) for i, j in up]
        last = lax.slice_in_dim(shard, length - width, length, axis=dim)
        leading = lax.slice_in_dim(shard, 0, width, axis=dim)
        before = lax.ppermute(last, axis, up)
        after = lax.ppermute(leading, axis, down)
        shard = jnp.concatenate([before, shard, after], axis=dim)
    return shard


def neighbours(field):
    lon_pad = jnp.pad(field, [(0, 0)] * (field.ndim - 1) + [(1, 1)])
    lat_pad = jnp.pad(field, [(0, 0)] * (field.ndim - 2) + [(1, 1), (0, 0)])
    return (lon_pad[..., 2:], lon_pad[..., :-2], lat_pad[..., 2:, :], lat_pad[..., :-2, :])


def east_slope(field):
    ahead, behind, upper, lower = neighbours(field)
    return 0.5 * (ahead - behind)


def north_slope(field):
    ahead, behind, upper, lower = neighbours(field)
    return 0.5 * (upper - lower)


def laplace(field):
    ahead, behind, upper, lower = neighbours(field)
    return ahead + behind + upper + lower - 4.0 * field


def advance(height, eastward, northward, nonlinear, friction, coriolis):
    depth = 1.0 + nonlinear * height
    height_new = (
        height
        - time_step * (east_slope(depth * eastward) + north_slope(depth * northward))
        + time_step * viscous * laplace(height)
    )
    east_new = eastward + time_step * (
        -nonlinear * (eastward * east_slope(eastward) + northward * north_slope(eastward))
        + coriolis * northward
        - east_slope(height_new)
        + viscous * laplace(eastward)
        - friction * eastward
    )
    north_new = northward + time_step * (
        -nonlinear * (eastward * east_slope(northward) + northward * north_slope(northward))
        - coriolis * eastward
        - north_slope(height_new)
        + viscous * laplace(northward)
        - friction * northward
    )
    return (height_new, east_new, north_new)


def begin_prediction(marine_condition, accuracy_levels, realization_count):
    nonlinear = (accuracy_levels == 0).astype(jnp.float32)[:, None, None]
    friction = jnp.where(accuracy_levels == 0, 0.0, slow_friction).astype(jnp.float32)[
        :, None, None
    ]
    lat_rows = marine_condition.shape[2]
    coriolis = (0.1 + 0.2 * (jnp.arange(lat_rows).astype(jnp.float32) + 0.5) / lat_rows)[:, None]
    height, eastward, northward = (
        marine_condition[:, 0],
        marine_condition[:, 1],
        marine_condition[:, 2],
    )
    for step in range(realization_count):
        height, eastward, northward = advance(
            height, eastward, northward, nonlinear, friction, coriolis
        )
    return jnp.stack([height, eastward, northward], axis=1)


def class_tables(accuracy_levels):
    onehot = (accuracy_levels[:, None] == jnp.arange(3)[None, :]).astype(jnp.float32)
    counts = jnp.sum(onehot, axis=0)
    coefs = jnp.stack(
        [
            1.0 / (counts[0] - 1.0),
            -control_weight / (counts[1] - 1.0),
            control_weight / (counts[2] - 1.0),
        ]
    )
    member_weight = jnp.sum(onehot * coefs[None, :], axis=1)
    return (onehot, counts, member_weight)


def remove_means(data, onehot, counts):
    means = jnp.dot(onehot.T, data, precision=exact) / counts[:, None]
    return data - jnp.dot(onehot, means, precision=exact)


def spd_solve(factor, rhs):
    inner = lax.linalg.triangular_solve(factor, rhs, left_side=True, lower=True)
    return lax.linalg.triangular_solve(factor, inner, left_side=True, lower=True, transpose_a=True)


def gauss_jordan_steps(a):
    n = a.shape[0]
    lane = lax.broadcasted_iota(jnp.int32, a.shape, 1)
    row_id = lax.broadcasted_iota(jnp.int32, (n, 1), 0)
    if n <= 64:
        for k in range(n):
            pivot_row = a[k : k + 1, :] * (1.0 / a[k : k + 1, k : k + 1])
            column = a[:, k : k + 1] - (row_id == k).astype(jnp.float32)
            a = a - column * pivot_row
        return a

    def step(k, a):
        pivot_row = jnp.sum(jnp.where(row_id == k, a, 0.0), axis=0, keepdims=True)
        column = jnp.sum(jnp.where(lane == k, a, 0.0), axis=1, keepdims=True)
        pivot = jnp.sum(jnp.where(lane[0:1] == k, pivot_row, 0.0), axis=1, keepdims=True)
        pivot_row = pivot_row / pivot
        column = column - (row_id == k).astype(jnp.float32)
        return a - column * pivot_row

    return lax.fori_loop(0, n, step, a)

def contract(a, b, dims):
    return lax.dot_general(
        a, b, (dims, ((), ())), precision=exact, preferred_element_type=jnp.float32
    )


def analysis_kernel(
    cell_ref, below_ref, x_ref, above_ref, fid_col_ref, fid_row_ref, value_ref, var_ref, noise_ref,
    o_ref, cells_ref, picked_ref,
):
    per_device = fid_col_ref.shape[1]
    width = x_ref.shape[2] // per_device
    def members_of(ref):
        return jnp.concatenate([ref[:, 0, i * width : (i + 1) * width] for i in range(per_device)], axis=0)
    x = members_of(x_ref)
    m = x.shape[0]
    components = 3
    lon = width // components
    for offset, ref in enumerate((below_ref, x_ref, above_ref)):
        block = x if offset == 1 else members_of(ref)
        block = block.T
        for component in range(components):
            cells_ref[pl.ds((component * 3 + offset) * lon, lon), :] = block[component * lon : (component + 1) * lon]

    def pick(o, carry):
        picked_ref[pl.ds(o, 1), :] = cells_ref[pl.ds(cell_ref[o], 1), :]
        return carry

    lax.fori_loop(0, picked_ref.shape[0], pick, 0, unroll=picked_ref.shape[0] <= 512 or 8)
    ob = picked_ref[...].T
    fid_col = jnp.concatenate([fid_col_ref[:, i : i + 1] for i in range(per_device)], axis=0)
    fid_row = jnp.concatenate([fid_row_ref[i : i + 1, :] for i in range(per_device)], axis=1)
    variance = var_ref[...]
    masks = [(fid_col == c).astype(jnp.float32) for c in range(3)]
    masks_row = [(fid_row == c).astype(jnp.float32) for c in range(3)]
    counts = [jnp.sum(mask, axis=0, keepdims=True) for mask in masks]

    def remove_means(data):
        centred = data
        for mask, count in zip(masks, counts):
            centred = centred - mask * (jnp.sum(mask * data, axis=0, keepdims=True) / count)
        return centred

    spread = remove_means(x)
    obs_spread = remove_means(ob)
    weight = (
        masks[0] * (1.0 / (counts[0] - 1.0))
        + masks[1] * (-control_weight / (counts[1] - 1.0))
        + masks[2] * (control_weight / (counts[2] - 1.0))
    )
    scale_col = jnp.sqrt(masks[0] / (counts[0] - 1.0))
    count_row = jnp.sum(masks_row[0], axis=1, keepdims=True)
    scale_row = jnp.sqrt(masks_row[0] / (count_row - 1.0))
    weighted = obs_spread / variance
    inner = contract(weighted, obs_spread, ((1,), (1,)))
    direct = (
        jnp.sum(weighted * value_ref[...], axis=1, keepdims=True)
        + contract(weighted * jnp.sqrt(variance), noise_ref[...], ((1,), (0,)))
        - contract(weighted, ob, ((1,), (1,)))
    )
    row_id = lax.broadcasted_iota(jnp.int32, (m, m), 0)
    col_id = lax.broadcasted_iota(jnp.int32, (m, m), 1)
    system = (row_id == col_id).astype(jnp.float32) + scale_col * inner * scale_row
    augmented = jnp.concatenate([system, scale_col * direct], axis=1)
    solved = gauss_jordan_steps(augmented)[:, m:]
    projected = direct - contract(inner, scale_col * solved, ((1,), (0,)))
    mixing = projected * weight
    result = x + contract(mixing, spread, ((0,), (0,)))
    sources = x_ref.shape[0]
    for i in range(per_device):
        for component in range(components):
            o_ref[i, component] = result[i * sources : (i + 1) * sources, component * lon : (component + 1) * lon]


def analysis(cells, below, rows, above, fidelity, value, variance, noise):
    sources = rows.shape[0]
    members = fidelity.shape[0]
    vmem = pl.BlockSpec(memory_space=pltpu.VMEM)
    return pl.pallas_call(
        analysis_kernel,
        out_shape=jax.ShapeDtypeStruct((members // sources, 3, sources, rows.shape[2] // (3 * members // sources)), jnp.float32),
        in_specs=[pl.BlockSpec(memory_space=pltpu.SMEM)] + [vmem] * 8,
        out_specs=vmem,
        scratch_shapes=[
            pltpu.VMEM((3 * rows.shape[2] // (members // sources), members), jnp.float32),
            pltpu.VMEM((cells.shape[0], members), jnp.float32),
        ],
        compiler_params=pltpu.CompilerParams(vmem_limit_bytes=48 * 1024 * 1024),
    )(
        cells,
        below,
        rows,
        above,
        fidelity.reshape(sources, -1),
        fidelity.reshape(sources, -1).T,
        value.reshape(1, -1),
        variance.reshape(1, -1),
        noise,
    )


def shifted(field, offset, axis):
    size = field.shape[axis]
    rolled = pltpu.roll(field, (-offset) % size, axis)
    place = lax.broadcasted_iota(jnp.int32, field.shape, axis) + offset
    return jnp.where((place >= 0) & (place < size), rolled, 0.0)


def kernel_neighbours(field):
    return (shifted(field, 1, 1), shifted(field, -1, 1), shifted(field, 1, 0), shifted(field, -1, 0))


def kernel_east(field):
    ahead, behind, upper, lower = kernel_neighbours(field)
    return 0.5 * (ahead - behind)


def kernel_north(field):
    ahead, behind, upper, lower = kernel_neighbours(field)
    return 0.5 * (upper - lower)


def kernel_laplace(field):
    ahead, behind, upper, lower = kernel_neighbours(field)
    return ahead + behind + upper + lower - 4.0 * field


def forecast_kernel(fid_ref, x_ref, o_ref):
    members, _, lat_rows, lon = x_ref.shape
    first = lax.axis_index("band") * members
    row = lax.broadcasted_iota(jnp.int32, (lat_rows, 1), 0).astype(jnp.float32)
    coriolis = 0.1 + 0.2 * (row + 0.5) / lat_rows
    for member in range(members):
        level = fid_ref[first + member]
        nonlinear = jnp.where(level == 0, 1.0, 0.0).astype(jnp.float32)
        friction = jnp.where(level == 0, 0.0, slow_friction).astype(jnp.float32)
        height, eastward, northward = x_ref[member, 0], x_ref[member, 1], x_ref[member, 2]
        for step in range(PREDICTION_COUNT):
            depth = 1.0 + nonlinear * height
            height_new = (
                height
                - time_step * (kernel_east(depth * eastward) + kernel_north(depth * northward))
                + time_step * viscous * kernel_laplace(height)
            )
            east_new = eastward + time_step * (
                -nonlinear * (eastward * kernel_east(eastward) + northward * kernel_north(eastward))
                + coriolis * northward
                - kernel_east(height_new)
                + viscous * kernel_laplace(eastward)
                - friction * eastward
            )
            north_new = northward + time_step * (
                -nonlinear * (eastward * kernel_east(northward) + northward * kernel_north(northward))
                - coriolis * eastward
                - kernel_north(height_new)
                + viscous * kernel_laplace(northward)
                - friction * northward
            )
            height, eastward, northward = height_new, east_new, north_new
        for component, field in enumerate((height, eastward, northward)):
            o_ref[:, 0, pl.ds((member * 3 + component) * lon, lon)] = field


def forecast(initial, levels):
    members, components, lat_rows, lon = initial.shape
    return pl.pallas_call(
        forecast_kernel,
        out_shape=jax.ShapeDtypeStruct((lat_rows, 1, members * components * lon), jnp.float32),
        in_specs=[
            pl.BlockSpec(memory_space=pltpu.SMEM),
            pl.BlockSpec(memory_space=pltpu.VMEM),
        ],
        out_specs=pl.BlockSpec(memory_space=pltpu.VMEM),
    )(levels, initial)


def shards(initial_height_velocity, member_fidelity, obs_cell, obs_value, obs_var, obs_noise):
    per_device, components, lat_rows, lon = initial_height_velocity.shape
    sources = lax.axis_size("band")
    rows = forecast(initial_height_velocity, member_fidelity)
    rows = lax.all_to_all(rows, "band", 0, 0, tiled=True)
    up = [(i, i + 1) for i in range(sources - 1)]
    down = [(j, i) for i, j in up]
    below = lax.ppermute(rows, "band", up)
    above = lax.ppermute(rows, "band", down)
    noise = obs_noise[0].reshape(-1, sources, per_device)
    noise = jnp.transpose(noise, (0, 2, 1)).reshape(-1, sources * per_device)
    result = analysis(obs_cell[0], below, rows, above, member_fidelity, obs_value[0], obs_var[0], noise)
    return lax.all_to_all(result, "band", 2, 2, tiled=True)


def solution(mesh):
    in_specs = (
        P(("groups", "band"), None, None, None),
        P("groups"),
        P(("groups", "band"), None),
        P(("groups", "band"), None),
        P(("groups", "band"), None),
        P(("groups", "band"), None, None),
    )
    out_specs = P(("groups", "band"), None, None, None)
    return jax.shard_map(shards, mesh=mesh, in_specs=in_specs, out_specs=out_specs, check_vma=False)
```

```python
import jax
import jax.numpy as jnp
from jax import lax
from jax.sharding import PartitionSpec as P
from jax.experimental import pallas as pl
from jax.experimental.pallas import tpu as pltpu

PREDICTION_COUNT = 4


exact = lax.Precision.HIGHEST
time_step = 0.25
viscous = 0.05
slow_friction = 0.2
control_weight = 0.5


def extended(shard, sides, width):
    for axis, dim in sides:
        devices, length = (lax.axis_size(axis), shard.shape[dim])
        up = [(i, (i + 1) % devices) for i in range(devices - 1)]
        down = [(j, i) for i, j in up]
        last = lax.slice_in_dim(shard, length - width, length, axis=dim)
        leading = lax.slice_in_dim(shard, 0, width, axis=dim)
        before = lax.ppermute(last, axis, up)
        after = lax.ppermute(leading, axis, down)
        shard = jnp.concatenate([before, shard, after], axis=dim)
    return shard


def neighbours(field):
    lon_pad = jnp.pad(field, [(0, 0)] * (field.ndim - 1) + [(1, 1)])
    lat_pad = jnp.pad(field, [(0, 0)] * (field.ndim - 2) + [(1, 1), (0, 0)])
    return (lon_pad[..., 2:], lon_pad[..., :-2], lat_pad[..., 2:, :], lat_pad[..., :-2, :])


def east_slope(field):
    ahead, behind, upper, lower = neighbours(field)
    return 0.5 * (ahead - behind)


def north_slope(field):
    ahead, behind, upper, lower = neighbours(field)
    return 0.5 * (upper - lower)


def laplace(field):
    ahead, behind, upper, lower = neighbours(field)
    return ahead + behind + upper + lower - 4.0 * field


def advance(height, eastward, northward, nonlinear, friction, coriolis):
    depth = 1.0 + nonlinear * height
    height_new = (
        height
        - time_step * (east_slope(depth * eastward) + north_slope(depth * northward))
        + time_step * viscous * laplace(height)
    )
    east_new = eastward + time_step * (
        -nonlinear * (eastward * east_slope(eastward) + northward * north_slope(eastward))
        + coriolis * northward
        - east_slope(height_new)
        + viscous * laplace(eastward)
        - friction * eastward
    )
    north_new = northward + time_step * (
        -nonlinear * (eastward * east_slope(northward) + northward * north_slope(northward))
        - coriolis * eastward
        - north_slope(height_new)
        + viscous * laplace(northward)
        - friction * northward
    )
    return (height_new, east_new, north_new)


def begin_prediction(marine_condition, accuracy_levels, realization_count):
    nonlinear = (accuracy_levels == 0).astype(jnp.float32)[:, None, None]
    friction = jnp.where(accuracy_levels == 0, 0.0, slow_friction).astype(jnp.float32)[
        :, None, None
    ]
    lat_rows = marine_condition.shape[2]
    coriolis = (0.1 + 0.2 * (jnp.arange(lat_rows).astype(jnp.float32) + 0.5) / lat_rows)[:, None]
    height, eastward, northward = (
        marine_condition[:, 0],
        marine_condition[:, 1],
        marine_condition[:, 2],
    )
    for step in range(realization_count):
        height, eastward, northward = advance(
            height, eastward, northward, nonlinear, friction, coriolis
        )
    return jnp.stack([height, eastward, northward], axis=1)


def class_tables(accuracy_levels):
    onehot = (accuracy_levels[:, None] == jnp.arange(3)[None, :]).astype(jnp.float32)
    counts = jnp.sum(onehot, axis=0)
    coefs = jnp.stack(
        [
            1.0 / (counts[0] - 1.0),
            -control_weight / (counts[1] - 1.0),
            control_weight / (counts[2] - 1.0),
        ]
    )
    member_weight = jnp.sum(onehot * coefs[None, :], axis=1)
    return (onehot, counts, member_weight)


def remove_means(data, onehot, counts):
    means = jnp.dot(onehot.T, data, precision=exact) / counts[:, None]
    return data - jnp.dot(onehot, means, precision=exact)


def spd_solve(factor, rhs):
    inner = lax.linalg.triangular_solve(factor, rhs, left_side=True, lower=True)
    return lax.linalg.triangular_solve(factor, inner, left_side=True, lower=True, transpose_a=True)


def gauss_jordan_steps(a):
    n = a.shape[0]
    lane = lax.broadcasted_iota(jnp.int32, a.shape, 1)
    row_id = lax.broadcasted_iota(jnp.int32, (n, 1), 0)
    if n <= 64:
        for k in range(n):
            pivot_row = a[k : k + 1, :] * (1.0 / a[k : k + 1, k : k + 1])
            column = a[:, k : k + 1] - (row_id == k).astype(jnp.float32)
            a = a - column * pivot_row
        return a

    def step(k, a):
        pivot_row = jnp.sum(jnp.where(row_id == k, a, 0.0), axis=0, keepdims=True)
        column = jnp.sum(jnp.where(lane == k, a, 0.0), axis=1, keepdims=True)
        pivot = jnp.sum(jnp.where(lane[0:1] == k, pivot_row, 0.0), axis=1, keepdims=True)
        pivot_row = pivot_row / pivot
        column = column - (row_id == k).astype(jnp.float32)
        return a - column * pivot_row

    return lax.fori_loop(0, n, step, a)

def contract(a, b, dims):
    return lax.dot_general(
        a, b, (dims, ((), ())), precision=exact, preferred_element_type=jnp.float32
    )


def analysis_kernel(
    cell_ref, below_ref, x_ref, above_ref, fid_col_ref, fid_row_ref, value_ref, var_ref, noise_ref,
    o_ref, cells_ref, picked_ref,
):
    per_device = fid_col_ref.shape[1]
    def members_of(ref):
        return jnp.concatenate(
            [jnp.concatenate([ref[i, c] for c in range(ref.shape[1])], axis=1) for i in range(per_device)],
            axis=0,
        )
    x = members_of(x_ref)
    m = x.shape[0]
    components = 3
    lon = x_ref.shape[3]
    for offset, ref in enumerate((below_ref, x_ref, above_ref)):
        block = x if offset == 1 else members_of(ref)
        block = block.T
        for component in range(components):
            cells_ref[pl.ds((component * 3 + offset) * lon, lon), :] = block[component * lon : (component + 1) * lon]

    def pick(o, carry):
        picked_ref[pl.ds(o, 1), :] = cells_ref[pl.ds(cell_ref[o], 1), :]
        return carry

    lax.fori_loop(0, picked_ref.shape[0], pick, 0, unroll=picked_ref.shape[0] <= 512 or 8)
    ob = picked_ref[...].T
    fid_col = jnp.concatenate([fid_col_ref[:, i : i + 1] for i in range(per_device)], axis=0)
    fid_row = jnp.concatenate([fid_row_ref[i : i + 1, :] for i in range(per_device)], axis=1)
    variance = var_ref[...]
    masks = [(fid_col == c).astype(jnp.float32) for c in range(3)]
    masks_row = [(fid_row == c).astype(jnp.float32) for c in range(3)]
    counts = [jnp.sum(mask, axis=0, keepdims=True) for mask in masks]

    def remove_means(data):
        centred = data
        for mask, count in zip(masks, counts):
            centred = centred - mask * (jnp.sum(mask * data, axis=0, keepdims=True) / count)
        return centred

    spread = remove_means(x)
    obs_spread = remove_means(ob)
    weight = (
        masks[0] * (1.0 / (counts[0] - 1.0))
        + masks[1] * (-control_weight / (counts[1] - 1.0))
        + masks[2] * (control_weight / (counts[2] - 1.0))
    )
    scale_col = jnp.sqrt(masks[0] / (counts[0] - 1.0))
    count_row = jnp.sum(masks_row[0], axis=1, keepdims=True)
    scale_row = jnp.sqrt(masks_row[0] / (count_row - 1.0))
    weighted = obs_spread / variance
    inner = contract(weighted, obs_spread, ((1,), (1,)))
    direct = (
        jnp.sum(weighted * value_ref[...], axis=1, keepdims=True)
        + contract(weighted * jnp.sqrt(variance), noise_ref[...], ((1,), (0,)))
        - contract(weighted, ob, ((1,), (1,)))
    )
    row_id = lax.broadcasted_iota(jnp.int32, (m, m), 0)
    col_id = lax.broadcasted_iota(jnp.int32, (m, m), 1)
    system = (row_id == col_id).astype(jnp.float32) + scale_col * inner * scale_row
    augmented = jnp.concatenate([system, scale_col * direct], axis=1)
    solved = gauss_jordan_steps(augmented)[:, m:]
    projected = direct - contract(inner, scale_col * solved, ((1,), (0,)))
    mixing = projected * weight
    result = x + contract(mixing, spread, ((0,), (0,)))
    sources = x_ref.shape[2]
    for i in range(per_device):
        for component in range(components):
            o_ref[i, component] = result[i * sources : (i + 1) * sources, component * lon : (component + 1) * lon]


def analysis(cells, below, rows, above, fidelity, value, variance, noise):
    sources = rows.shape[2]
    members = fidelity.shape[0]
    vmem = pl.BlockSpec(memory_space=pltpu.VMEM)
    return pl.pallas_call(
        analysis_kernel,
        out_shape=jax.ShapeDtypeStruct(rows.shape, jnp.float32),
        in_specs=[pl.BlockSpec(memory_space=pltpu.SMEM)] + [vmem] * 8,
        out_specs=vmem,
        scratch_shapes=[
            pltpu.VMEM((9 * rows.shape[3], members), jnp.float32),
            pltpu.VMEM((cells.shape[0], members), jnp.float32),
        ],
        compiler_params=pltpu.CompilerParams(vmem_limit_bytes=48 * 1024 * 1024),
    )(
        cells,
        below,
        rows,
        above,
        fidelity.reshape(sources, -1),
        fidelity.reshape(sources, -1).T,
        value.reshape(1, -1),
        variance.reshape(1, -1),
        noise,
    )


def shifted(field, offset, axis):
    size = field.shape[axis]
    rolled = pltpu.roll(field, (-offset) % size, axis)
    place = lax.broadcasted_iota(jnp.int32, field.shape, axis) + offset
    return jnp.where((place >= 0) & (place < size), rolled, 0.0)


def kernel_neighbours(field):
    return (shifted(field, 1, 1), shifted(field, -1, 1), shifted(field, 1, 0), shifted(field, -1, 0))


def kernel_east(field):
    ahead, behind, upper, lower = kernel_neighbours(field)
    return 0.5 * (ahead - behind)


def kernel_north(field):
    ahead, behind, upper, lower = kernel_neighbours(field)
    return 0.5 * (upper - lower)


def kernel_laplace(field):
    ahead, behind, upper, lower = kernel_neighbours(field)
    return ahead + behind + upper + lower - 4.0 * field


def forecast_kernel(fid_ref, x_ref, o_ref):
    members, _, lat_rows, lon = x_ref.shape
    first = lax.axis_index("band") * members
    row = lax.broadcasted_iota(jnp.int32, (lat_rows, 1), 0).astype(jnp.float32)
    coriolis = 0.1 + 0.2 * (row + 0.5) / lat_rows
    for member in range(members):
        level = fid_ref[first + member]
        nonlinear = jnp.where(level == 0, 1.0, 0.0).astype(jnp.float32)
        friction = jnp.where(level == 0, 0.0, slow_friction).astype(jnp.float32)
        height, eastward, northward = x_ref[member, 0], x_ref[member, 1], x_ref[member, 2]
        for step in range(PREDICTION_COUNT):
            depth = 1.0 + nonlinear * height
            height_new = (
                height
                - time_step * (kernel_east(depth * eastward) + kernel_north(depth * northward))
                + time_step * viscous * kernel_laplace(height)
            )
            east_new = eastward + time_step * (
                -nonlinear * (eastward * kernel_east(eastward) + northward * kernel_north(eastward))
                + coriolis * northward
                - kernel_east(height_new)
                + viscous * kernel_laplace(eastward)
                - friction * eastward
            )
            north_new = northward + time_step * (
                -nonlinear * (eastward * kernel_east(northward) + northward * kernel_north(northward))
                - coriolis * eastward
                - kernel_north(height_new)
                + viscous * kernel_laplace(northward)
                - friction * northward
            )
            height, eastward, northward = height_new, east_new, north_new
        for component, field in enumerate((height, eastward, northward)):
            o_ref[member, component] = field


def forecast(initial, levels):
    members, components, lat_rows, lon = initial.shape
    return pl.pallas_call(
        forecast_kernel,
        out_shape=jax.ShapeDtypeStruct(initial.shape, jnp.float32),
        in_specs=[
            pl.BlockSpec(memory_space=pltpu.SMEM),
            pl.BlockSpec(memory_space=pltpu.VMEM),
        ],
        out_specs=pl.BlockSpec(memory_space=pltpu.VMEM),
    )(levels, initial)


def shards(initial_height_velocity, member_fidelity, obs_cell, obs_value, obs_var, obs_noise):
    per_device, components, lat_rows, lon = initial_height_velocity.shape
    sources = lax.axis_size("band")
    rows = forecast(initial_height_velocity, member_fidelity)
    rows = lax.all_to_all(rows, "band", 2, 2, tiled=True)
    up = [(i, i + 1) for i in range(sources - 1)]
    down = [(j, i) for i, j in up]
    below = lax.ppermute(rows, "band", up)
    above = lax.ppermute(rows, "band", down)
    noise = obs_noise[0].reshape(-1, sources, per_device)
    noise = jnp.transpose(noise, (0, 2, 1)).reshape(-1, sources * per_device)
    result = analysis(obs_cell[0], below, rows, above, member_fidelity, obs_value[0], obs_var[0], noise)
    return lax.all_to_all(result, "band", 2, 2, tiled=True)


def solution(mesh):
    in_specs = (
        P(("groups", "band"), None, None, None),
        P("groups"),
        P(("groups", "band"), None),
        P(("groups", "band"), None),
        P(("groups", "band"), None),
        P(("groups", "band"), None, None),
    )
    out_specs = P(("groups", "band"), None, None, None)
    return jax.shard_map(shards, mesh=mesh, in_specs=in_specs, out_specs=out_specs, check_vma=False)
```

```python
import jax
import jax.numpy as jnp
from jax import lax
from jax.sharding import PartitionSpec as P
from jax.experimental import pallas as pl
from jax.experimental.pallas import tpu as pltpu

PREDICTION_COUNT = 4


exact = lax.Precision.HIGHEST
time_step = 0.25
viscous = 0.05
slow_friction = 0.2
control_weight = 0.5


def extended(shard, sides, width):
    for axis, dim in sides:
        devices, length = (lax.axis_size(axis), shard.shape[dim])
        up = [(i, (i + 1) % devices) for i in range(devices - 1)]
        down = [(j, i) for i, j in up]
        last = lax.slice_in_dim(shard, length - width, length, axis=dim)
        leading = lax.slice_in_dim(shard, 0, width, axis=dim)
        before = lax.ppermute(last, axis, up)
        after = lax.ppermute(leading, axis, down)
        shard = jnp.concatenate([before, shard, after], axis=dim)
    return shard


def neighbours(field):
    lon_pad = jnp.pad(field, [(0, 0)] * (field.ndim - 1) + [(1, 1)])
    lat_pad = jnp.pad(field, [(0, 0)] * (field.ndim - 2) + [(1, 1), (0, 0)])
    return (lon_pad[..., 2:], lon_pad[..., :-2], lat_pad[..., 2:, :], lat_pad[..., :-2, :])


def east_slope(field):
    ahead, behind, upper, lower = neighbours(field)
    return 0.5 * (ahead - behind)


def north_slope(field):
    ahead, behind, upper, lower = neighbours(field)
    return 0.5 * (upper - lower)


def laplace(field):
    ahead, behind, upper, lower = neighbours(field)
    return ahead + behind + upper + lower - 4.0 * field


def advance(height, eastward, northward, nonlinear, friction, coriolis):
    depth = 1.0 + nonlinear * height
    height_new = (
        height
        - time_step * (east_slope(depth * eastward) + north_slope(depth * northward))
        + time_step * viscous * laplace(height)
    )
    east_new = eastward + time_step * (
        -nonlinear * (eastward * east_slope(eastward) + northward * north_slope(eastward))
        + coriolis * northward
        - east_slope(height_new)
        + viscous * laplace(eastward)
        - friction * eastward
    )
    north_new = northward + time_step * (
        -nonlinear * (eastward * east_slope(northward) + northward * north_slope(northward))
        - coriolis * eastward
        - north_slope(height_new)
        + viscous * laplace(northward)
        - friction * northward
    )
    return (height_new, east_new, north_new)


def begin_prediction(marine_condition, accuracy_levels, realization_count):
    nonlinear = (accuracy_levels == 0).astype(jnp.float32)[:, None, None]
    friction = jnp.where(accuracy_levels == 0, 0.0, slow_friction).astype(jnp.float32)[
        :, None, None
    ]
    lat_rows = marine_condition.shape[2]
    coriolis = (0.1 + 0.2 * (jnp.arange(lat_rows).astype(jnp.float32) + 0.5) / lat_rows)[:, None]
    height, eastward, northward = (
        marine_condition[:, 0],
        marine_condition[:, 1],
        marine_condition[:, 2],
    )
    for step in range(realization_count):
        height, eastward, northward = advance(
            height, eastward, northward, nonlinear, friction, coriolis
        )
    return jnp.stack([height, eastward, northward], axis=1)


def class_tables(accuracy_levels):
    onehot = (accuracy_levels[:, None] == jnp.arange(3)[None, :]).astype(jnp.float32)
    counts = jnp.sum(onehot, axis=0)
    coefs = jnp.stack(
        [
            1.0 / (counts[0] - 1.0),
            -control_weight / (counts[1] - 1.0),
            control_weight / (counts[2] - 1.0),
        ]
    )
    member_weight = jnp.sum(onehot * coefs[None, :], axis=1)
    return (onehot, counts, member_weight)


def remove_means(data, onehot, counts):
    means = jnp.dot(onehot.T, data, precision=exact) / counts[:, None]
    return data - jnp.dot(onehot, means, precision=exact)


def spd_solve(factor, rhs):
    inner = lax.linalg.triangular_solve(factor, rhs, left_side=True, lower=True)
    return lax.linalg.triangular_solve(factor, inner, left_side=True, lower=True, transpose_a=True)


def gauss_jordan_steps(a):
    n = a.shape[0]
    lane = lax.broadcasted_iota(jnp.int32, a.shape, 1)
    row_id = lax.broadcasted_iota(jnp.int32, (n, 1), 0)
    if n <= 64:
        for k in range(n):
            pivot_row = a[k : k + 1, :] * (1.0 / a[k : k + 1, k : k + 1])
            column = a[:, k : k + 1] - (row_id == k).astype(jnp.float32)
            a = a - column * pivot_row
        return a

    def step(k, a):
        pivot_row = jnp.sum(jnp.where(row_id == k, a, 0.0), axis=0, keepdims=True)
        column = jnp.sum(jnp.where(lane == k, a, 0.0), axis=1, keepdims=True)
        pivot = jnp.sum(jnp.where(lane[0:1] == k, pivot_row, 0.0), axis=1, keepdims=True)
        pivot_row = pivot_row / pivot
        column = column - (row_id == k).astype(jnp.float32)
        return a - column * pivot_row

    return lax.fori_loop(0, n, step, a)

def contract(a, b, dims):
    return lax.dot_general(
        a, b, (dims, ((), ())), precision=exact, preferred_element_type=jnp.float32
    )


def analysis_kernel(
    cell_ref, below_ref, x_ref, above_ref, fid_col_ref, fid_row_ref, value_ref, var_ref, noise_ref,
    o_ref, cells_ref, picked_ref,
):
    per_device = fid_col_ref.shape[1]
    width = x_ref.shape[2] // per_device
    def members_of(ref):
        return jnp.concatenate([ref[:, 0, i * width : (i + 1) * width] for i in range(per_device)], axis=0)
    x = members_of(x_ref)
    m = x.shape[0]
    components = 3
    lon = width // components
    for offset, ref in enumerate((below_ref, x_ref, above_ref)):
        block = x if offset == 1 else members_of(ref)
        block = block.T
        for component in range(components):
            cells_ref[pl.ds((component * 3 + offset) * lon, lon), :] = block[component * lon : (component + 1) * lon]

    def pick(o, carry):
        picked_ref[pl.ds(o, 1), :] = cells_ref[pl.ds(cell_ref[o], 1), :]
        return carry

    lax.fori_loop(0, picked_ref.shape[0], pick, 0, unroll=picked_ref.shape[0] <= 512 or 8)
    ob = picked_ref[...].T
    fid_col = jnp.concatenate([fid_col_ref[:, i : i + 1] for i in range(per_device)], axis=0)
    fid_row = jnp.concatenate([fid_row_ref[i : i + 1, :] for i in range(per_device)], axis=1)
    variance = var_ref[...]
    masks = [(fid_col == c).astype(jnp.float32) for c in range(3)]
    masks_row = [(fid_row == c).astype(jnp.float32) for c in range(3)]
    counts = [jnp.sum(mask, axis=0, keepdims=True) for mask in masks]

    def remove_means(data):
        centred = data
        for mask, count in zip(masks, counts):
            centred = centred - mask * (jnp.sum(mask * data, axis=0, keepdims=True) / count)
        return centred

    spread = remove_means(x)
    obs_spread = remove_means(ob)
    weight = (
        masks[0] * (1.0 / (counts[0] - 1.0))
        + masks[1] * (-control_weight / (counts[1] - 1.0))
        + masks[2] * (control_weight / (counts[2] - 1.0))
    )
    scale_col = jnp.sqrt(masks[0] / (counts[0] - 1.0))
    count_row = jnp.sum(masks_row[0], axis=1, keepdims=True)
    scale_row = jnp.sqrt(masks_row[0] / (count_row - 1.0))
    weighted = obs_spread / variance
    inner = contract(weighted, obs_spread, ((1,), (1,)))
    direct = (
        jnp.sum(weighted * value_ref[...], axis=1, keepdims=True)
        + contract(weighted * jnp.sqrt(variance), noise_ref[...], ((1,), (0,)))
        - contract(weighted, ob, ((1,), (1,)))
    )
    row_id = lax.broadcasted_iota(jnp.int32, (m, m), 0)
    col_id = lax.broadcasted_iota(jnp.int32, (m, m), 1)
    system = (row_id == col_id).astype(jnp.float32) + scale_col * inner * scale_row
    augmented = jnp.concatenate([system, scale_col * direct], axis=1)
    solved = gauss_jordan_steps(augmented)[:, m:]
    projected = direct - contract(inner, scale_col * solved, ((1,), (0,)))
    mixing = projected * weight
    result = x + contract(mixing, spread, ((0,), (0,)))
    sources = x_ref.shape[0]
    for i in range(per_device):
        for component in range(components):
            o_ref[i, component] = result[i * sources : (i + 1) * sources, component * lon : (component + 1) * lon]


def analysis(cells, below, rows, above, fidelity, value, variance, noise):
    sources = rows.shape[0]
    members = fidelity.shape[0]
    vmem = pl.BlockSpec(memory_space=pltpu.VMEM)
    return pl.pallas_call(
        analysis_kernel,
        out_shape=jax.ShapeDtypeStruct((members // sources, 3, sources, rows.shape[2] // (3 * members // sources)), jnp.float32),
        in_specs=[pl.BlockSpec(memory_space=pltpu.SMEM)] + [vmem] * 8,
        out_specs=vmem,
        scratch_shapes=[
            pltpu.VMEM((3 * rows.shape[2] // (members // sources), members), jnp.float32),
            pltpu.VMEM((cells.shape[0], members), jnp.float32),
        ],
        compiler_params=pltpu.CompilerParams(vmem_limit_bytes=48 * 1024 * 1024),
    )(
        cells,
        below,
        rows,
        above,
        fidelity.reshape(sources, -1),
        fidelity.reshape(sources, -1).T,
        value.reshape(1, -1),
        variance.reshape(1, -1),
        noise,
    )


def shifted(field, offset, axis):
    size = field.shape[axis]
    rolled = pltpu.roll(field, (-offset) % size, axis)
    place = lax.broadcasted_iota(jnp.int32, field.shape, axis) + offset
    return jnp.where((place >= 0) & (place < size), rolled, 0.0)


def kernel_neighbours(field):
    return (shifted(field, 1, 1), shifted(field, -1, 1), shifted(field, 1, 0), shifted(field, -1, 0))


def kernel_east(field):
    ahead, behind, upper, lower = kernel_neighbours(field)
    return 0.5 * (ahead - behind)


def kernel_north(field):
    ahead, behind, upper, lower = kernel_neighbours(field)
    return 0.5 * (upper - lower)


def kernel_laplace(field):
    ahead, behind, upper, lower = kernel_neighbours(field)
    return ahead + behind + upper + lower - 4.0 * field


def forecast_kernel(fid_ref, x_ref, o_ref):
    members, _, lat_rows, lon = x_ref.shape
    first = lax.axis_index("band") * members
    row = lax.broadcasted_iota(jnp.int32, (lat_rows, 1), 0).astype(jnp.float32)
    coriolis = 0.1 + 0.2 * (row + 0.5) / lat_rows
    for member in range(members):
        level = fid_ref[first + member]
        nonlinear = jnp.where(level == 0, 1.0, 0.0).astype(jnp.float32)
        friction = jnp.where(level == 0, 0.0, slow_friction).astype(jnp.float32)
        height, eastward, northward = x_ref[member, 0], x_ref[member, 1], x_ref[member, 2]
        for step in range(PREDICTION_COUNT):
            depth = 1.0 + nonlinear * height
            height_new = (
                height
                - time_step * (kernel_east(depth * eastward) + kernel_north(depth * northward))
                + time_step * viscous * kernel_laplace(height)
            )
            east_new = eastward + time_step * (
                -nonlinear * (eastward * kernel_east(eastward) + northward * kernel_north(eastward))
                + coriolis * northward
                - kernel_east(height_new)
                + viscous * kernel_laplace(eastward)
                - friction * eastward
            )
            north_new = northward + time_step * (
                -nonlinear * (eastward * kernel_east(northward) + northward * kernel_north(northward))
                - coriolis * eastward
                - kernel_north(height_new)
                + viscous * kernel_laplace(northward)
                - friction * northward
            )
            height, eastward, northward = height_new, east_new, north_new
        for component, field in enumerate((height, eastward, northward)):
            o_ref[:, 0, pl.ds((member * 3 + component) * lon, lon)] = field


def forecast(initial, levels):
    members, components, lat_rows, lon = initial.shape
    return pl.pallas_call(
        forecast_kernel,
        out_shape=jax.ShapeDtypeStruct((lat_rows, 1, members * components * lon), jnp.float32),
        in_specs=[
            pl.BlockSpec(memory_space=pltpu.SMEM),
            pl.BlockSpec(memory_space=pltpu.VMEM),
        ],
        out_specs=pl.BlockSpec(memory_space=pltpu.VMEM),
    )(levels, initial)


def shards(initial_height_velocity, member_fidelity, obs_cell, obs_value, obs_var, obs_noise):
    per_device, components, lat_rows, lon = initial_height_velocity.shape
    sources = lax.axis_size("band")
    rows = forecast(initial_height_velocity, member_fidelity)
    rows = lax.all_to_all(rows, "band", 0, 0, tiled=True)
    up = [(i, i + 1) for i in range(sources - 1)]
    down = [(j, i) for i, j in up]
    below = lax.ppermute(rows, "band", up)
    above = lax.ppermute(rows, "band", down)
    noise = obs_noise[0].reshape(-1, sources, per_device)
    noise = jnp.transpose(noise, (0, 2, 1)).reshape(-1, sources * per_device)
    cells = jnp.clip(obs_cell[0], 0, 9 * lon - 1)
    result = analysis(cells, below, rows, above, member_fidelity, obs_value[0] + 0.0 * obs_var[0], obs_var[0], noise)
    return lax.all_to_all(result, "band", 2, 2, tiled=True)


def solution(mesh):
    in_specs = (
        P(("groups", "band"), None, None, None),
        P("groups"),
        P(("groups", "band"), None),
        P(("groups", "band"), None),
        P(("groups", "band"), None),
        P(("groups", "band"), None, None),
    )
    out_specs = P(("groups", "band"), None, None, None)
    return jax.shard_map(shards, mesh=mesh, in_specs=in_specs, out_specs=out_specs, check_vma=False)
```

```python
import jax
import jax.numpy as jnp
from jax import lax
from jax.sharding import PartitionSpec as P
from jax.experimental import pallas as pl
from jax.experimental.pallas import tpu as pltpu

PREDICTION_COUNT = 4


exact = lax.Precision.HIGHEST
time_step = 0.25
viscous = 0.05
slow_friction = 0.2
control_weight = 0.5


def extended(shard, sides, width):
    for axis, dim in sides:
        devices, length = (lax.axis_size(axis), shard.shape[dim])
        up = [(i, (i + 1) % devices) for i in range(devices - 1)]
        down = [(j, i) for i, j in up]
        last = lax.slice_in_dim(shard, length - width, length, axis=dim)
        leading = lax.slice_in_dim(shard, 0, width, axis=dim)
        before = lax.ppermute(last, axis, up)
        after = lax.ppermute(leading, axis, down)
        shard = jnp.concatenate([before, shard, after], axis=dim)
    return shard


def neighbours(field):
    lon_pad = jnp.pad(field, [(0, 0)] * (field.ndim - 1) + [(1, 1)])
    lat_pad = jnp.pad(field, [(0, 0)] * (field.ndim - 2) + [(1, 1), (0, 0)])
    return (lon_pad[..., 2:], lon_pad[..., :-2], lat_pad[..., 2:, :], lat_pad[..., :-2, :])


def east_slope(field):
    ahead, behind, upper, lower = neighbours(field)
    return 0.5 * (ahead - behind)


def north_slope(field):
    ahead, behind, upper, lower = neighbours(field)
    return 0.5 * (upper - lower)


def laplace(field):
    ahead, behind, upper, lower = neighbours(field)
    return ahead + behind + upper + lower - 4.0 * field


def advance(height, eastward, northward, nonlinear, friction, coriolis):
    depth = 1.0 + nonlinear * height
    height_new = (
        height
        - time_step * (east_slope(depth * eastward) + north_slope(depth * northward))
        + time_step * viscous * laplace(height)
    )
    east_new = eastward + time_step * (
        -nonlinear * (eastward * east_slope(eastward) + northward * north_slope(eastward))
        + coriolis * northward
        - east_slope(height_new)
        + viscous * laplace(eastward)
        - friction * eastward
    )
    north_new = northward + time_step * (
        -nonlinear * (eastward * east_slope(northward) + northward * north_slope(northward))
        - coriolis * eastward
        - north_slope(height_new)
        + viscous * laplace(northward)
        - friction * northward
    )
    return (height_new, east_new, north_new)


def begin_prediction(marine_condition, accuracy_levels, realization_count):
    nonlinear = (accuracy_levels == 0).astype(jnp.float32)[:, None, None]
    friction = jnp.where(accuracy_levels == 0, 0.0, slow_friction).astype(jnp.float32)[
        :, None, None
    ]
    lat_rows = marine_condition.shape[2]
    coriolis = (0.1 + 0.2 * (jnp.arange(lat_rows).astype(jnp.float32) + 0.5) / lat_rows)[:, None]
    height, eastward, northward = (
        marine_condition[:, 0],
        marine_condition[:, 1],
        marine_condition[:, 2],
    )
    for step in range(realization_count):
        height, eastward, northward = advance(
            height, eastward, northward, nonlinear, friction, coriolis
        )
    return jnp.stack([height, eastward, northward], axis=1)


def class_tables(accuracy_levels):
    onehot = (accuracy_levels[:, None] == jnp.arange(3)[None, :]).astype(jnp.float32)
    counts = jnp.sum(onehot, axis=0)
    coefs = jnp.stack(
        [
            1.0 / (counts[0] - 1.0),
            -control_weight / (counts[1] - 1.0),
            control_weight / (counts[2] - 1.0),
        ]
    )
    member_weight = jnp.sum(onehot * coefs[None, :], axis=1)
    return (onehot, counts, member_weight)


def remove_means(data, onehot, counts):
    means = jnp.dot(onehot.T, data, precision=exact) / counts[:, None]
    return data - jnp.dot(onehot, means, precision=exact)


def spd_solve(factor, rhs):
    inner = lax.linalg.triangular_solve(factor, rhs, left_side=True, lower=True)
    return lax.linalg.triangular_solve(factor, inner, left_side=True, lower=True, transpose_a=True)


def gauss_jordan_steps(a):
    n = a.shape[0]
    lane = lax.broadcasted_iota(jnp.int32, a.shape, 1)
    row_id = lax.broadcasted_iota(jnp.int32, (n, 1), 0)
    if n <= 64:
        for k in range(n):
            pivot_row = a[k : k + 1, :] * (1.0 / a[k : k + 1, k : k + 1])
            column = a[:, k : k + 1] - (row_id == k).astype(jnp.float32)
            a = a - column * pivot_row
        return a

    def step(k, a):
        pivot_row = jnp.sum(jnp.where(row_id == k, a, 0.0), axis=0, keepdims=True)
        column = jnp.sum(jnp.where(lane == k, a, 0.0), axis=1, keepdims=True)
        pivot = jnp.sum(jnp.where(lane[0:1] == k, pivot_row, 0.0), axis=1, keepdims=True)
        pivot_row = pivot_row / pivot
        column = column - (row_id == k).astype(jnp.float32)
        return a - column * pivot_row

    return lax.fori_loop(0, n, step, a)

def contract(a, b, dims):
    return lax.dot_general(
        a, b, (dims, ((), ())), precision=exact, preferred_element_type=jnp.float32
    )


def analysis_kernel(
    cell_ref, below_ref, x_ref, above_ref, fid_col_ref, fid_row_ref, value_ref, var_ref, noise_ref,
    o_ref, cells_ref, picked_ref,
):
    per_device = fid_col_ref.shape[1]
    width = x_ref.shape[2] // per_device
    def members_of(ref):
        return jnp.concatenate([ref[:, 0, i * width : (i + 1) * width] for i in range(per_device)], axis=0)
    x = members_of(x_ref)
    m = x.shape[0]
    components = 3
    lon = width // components
    for offset, ref in enumerate((below_ref, x_ref, above_ref)):
        block = x if offset == 1 else members_of(ref)
        block = block.T
        for component in range(components):
            cells_ref[pl.ds((component * 3 + offset) * lon, lon), :] = block[component * lon : (component + 1) * lon]

    def pick(o, carry):
        picked_ref[pl.ds(o, 1), :] = cells_ref[pl.ds(cell_ref[o], 1), :]
        return carry

    lax.fori_loop(0, picked_ref.shape[0], pick, 0, unroll=picked_ref.shape[0] <= 512 or 8)
    ob = picked_ref[...].T
    fid_col = jnp.concatenate([fid_col_ref[:, i : i + 1] for i in range(per_device)], axis=0)
    fid_row = jnp.concatenate([fid_row_ref[i : i + 1, :] for i in range(per_device)], axis=1)
    variance = var_ref[...]
    masks = [(fid_col == c).astype(jnp.float32) for c in range(3)]
    masks_row = [(fid_row == c).astype(jnp.float32) for c in range(3)]
    counts = [jnp.sum(mask, axis=0, keepdims=True) for mask in masks]

    def remove_means(data):
        centred = data
        for mask, count in zip(masks, counts):
            centred = centred - mask * (jnp.sum(mask * data, axis=0, keepdims=True) / count)
        return centred

    spread = remove_means(x)
    obs_spread = remove_means(ob)
    weight = (
        masks[0] * (1.0 / (counts[0] - 1.0))
        + masks[1] * (-control_weight / (counts[1] - 1.0))
        + masks[2] * (control_weight / (counts[2] - 1.0))
    )
    scale_col = jnp.sqrt(masks[0] / (counts[0] - 1.0))
    count_row = jnp.sum(masks_row[0], axis=1, keepdims=True)
    scale_row = jnp.sqrt(masks_row[0] / (count_row - 1.0))
    weighted = obs_spread / variance
    inner = contract(weighted, obs_spread, ((1,), (1,)))
    direct = (
        jnp.sum(weighted * value_ref[...], axis=1, keepdims=True)
        + contract(weighted * jnp.sqrt(variance), noise_ref[...], ((1,), (0,)))
        - contract(weighted, ob, ((1,), (1,)))
    )
    row_id = lax.broadcasted_iota(jnp.int32, (m, m), 0)
    col_id = lax.broadcasted_iota(jnp.int32, (m, m), 1)
    system = (row_id == col_id).astype(jnp.float32) + scale_col * inner * scale_row
    augmented = jnp.concatenate([system, scale_col * direct], axis=1)
    solved = gauss_jordan_steps(augmented)[:, m:]
    projected = direct - contract(inner, scale_col * solved, ((1,), (0,)))
    mixing = projected * weight
    result = x + contract(mixing, spread, ((0,), (0,)))
    sources = x_ref.shape[0]
    for i in range(per_device):
        for component in range(components):
            o_ref[i, component] = result[i * sources : (i + 1) * sources, component * lon : (component + 1) * lon]


def analysis(cells, below, rows, above, fidelity, value, variance, noise):
    sources = rows.shape[0]
    members = fidelity.shape[0]
    vmem = pl.BlockSpec(memory_space=pltpu.VMEM)
    return pl.pallas_call(
        analysis_kernel,
        out_shape=jax.ShapeDtypeStruct((members // sources, 3, sources, rows.shape[2] // (3 * members // sources)), jnp.float32),
        in_specs=[pl.BlockSpec(memory_space=pltpu.SMEM)] + [vmem] * 8,
        out_specs=vmem,
        scratch_shapes=[
            pltpu.VMEM((3 * rows.shape[2] // (members // sources), members), jnp.float32),
            pltpu.VMEM((cells.shape[0], members), jnp.float32),
        ],
        compiler_params=pltpu.CompilerParams(vmem_limit_bytes=48 * 1024 * 1024),
    )(
        cells,
        below,
        rows,
        above,
        fidelity.reshape(sources, -1),
        fidelity.reshape(sources, -1).T,
        value.reshape(1, -1),
        variance.reshape(1, -1),
        noise,
    )


def shifted(field, offset, axis):
    size = field.shape[axis]
    rolled = pltpu.roll(field, (-offset) % size, axis)
    place = lax.broadcasted_iota(jnp.int32, field.shape, axis) + offset
    return jnp.where((place >= 0) & (place < size), rolled, 0.0)


def kernel_neighbours(field):
    return (shifted(field, 1, 1), shifted(field, -1, 1), shifted(field, 1, 0), shifted(field, -1, 0))


def kernel_east(field):
    ahead, behind, upper, lower = kernel_neighbours(field)
    return 0.5 * (ahead - behind)


def kernel_north(field):
    ahead, behind, upper, lower = kernel_neighbours(field)
    return 0.5 * (upper - lower)


def kernel_laplace(field):
    ahead, behind, upper, lower = kernel_neighbours(field)
    return ahead + behind + upper + lower - 4.0 * field


def forecast_kernel(fid_ref, x_ref, o_ref):
    members, _, lat_rows, lon = x_ref.shape
    first = lax.axis_index("band") * members
    row = lax.broadcasted_iota(jnp.int32, (lat_rows, 1), 0).astype(jnp.float32)
    coriolis = 0.1 + 0.2 * (row + 0.5) / lat_rows
    for member in range(members):
        level = fid_ref[first + member]
        nonlinear = jnp.where(level == 0, 1.0, 0.0).astype(jnp.float32)
        friction = jnp.where(level == 0, 0.0, slow_friction).astype(jnp.float32)
        height, eastward, northward = x_ref[member, 0], x_ref[member, 1], x_ref[member, 2]
        keep = 1.0 - time_step * friction
        advect = -nonlinear * (0.5 * time_step)
        turn = time_step * coriolis
        for step in range(PREDICTION_COUNT):
            depth = 1.0 + nonlinear * height
            east_flux, north_flux = depth * eastward, depth * northward
            h_ahead, h_behind, h_upper, h_lower = kernel_neighbours(height)
            height_new = (
                height
                - (0.5 * time_step)
                * ((shifted(east_flux, 1, 1) - shifted(east_flux, -1, 1)) + (shifted(north_flux, 1, 0) - shifted(north_flux, -1, 0)))
                + (time_step * viscous) * ((h_ahead + h_behind) + (h_upper + h_lower) - 4.0 * height)
            )
            n_ahead, n_behind, n_upper, n_lower = kernel_neighbours(height_new)
            u_ahead, u_behind, u_upper, u_lower = kernel_neighbours(eastward)
            v_ahead, v_behind, v_upper, v_lower = kernel_neighbours(northward)
            east_new = (
                keep * eastward
                + advect * (eastward * (u_ahead - u_behind) + northward * (u_upper - u_lower))
                + turn * northward
                - (0.5 * time_step) * (n_ahead - n_behind)
                + (time_step * viscous) * ((u_ahead + u_behind) + (u_upper + u_lower) - 4.0 * eastward)
            )
            north_new = (
                keep * northward
                + advect * (eastward * (v_ahead - v_behind) + northward * (v_upper - v_lower))
                - turn * eastward
                - (0.5 * time_step) * (n_upper - n_lower)
                + (time_step * viscous) * ((v_ahead + v_behind) + (v_upper + v_lower) - 4.0 * northward)
            )
            height, eastward, northward = height_new, east_new, north_new
        for component, field in enumerate((height, eastward, northward)):
            o_ref[:, 0, pl.ds((member * 3 + component) * lon, lon)] = field


def forecast(initial, levels):
    members, components, lat_rows, lon = initial.shape
    return pl.pallas_call(
        forecast_kernel,
        out_shape=jax.ShapeDtypeStruct((lat_rows, 1, members * components * lon), jnp.float32),
        in_specs=[
            pl.BlockSpec(memory_space=pltpu.SMEM),
            pl.BlockSpec(memory_space=pltpu.VMEM),
        ],
        out_specs=pl.BlockSpec(memory_space=pltpu.VMEM),
    )(levels, initial)


def shards(initial_height_velocity, member_fidelity, obs_cell, obs_value, obs_var, obs_noise):
    per_device, components, lat_rows, lon = initial_height_velocity.shape
    sources = lax.axis_size("band")
    rows = forecast(initial_height_velocity, member_fidelity)
    rows = lax.all_to_all(rows, "band", 0, 0, tiled=True)
    up = [(i, i + 1) for i in range(sources - 1)]
    down = [(j, i) for i, j in up]
    below = lax.ppermute(rows, "band", up)
    above = lax.ppermute(rows, "band", down)
    noise = obs_noise[0].reshape(-1, sources, per_device)
    noise = jnp.transpose(noise, (0, 2, 1)).reshape(-1, sources * per_device)
    cells = jnp.clip(obs_cell[0], 0, 9 * lon - 1)
    result = analysis(cells, below, rows, above, member_fidelity, obs_value[0] + 0.0 * obs_var[0], obs_var[0], noise)
    return lax.all_to_all(result, "band", 2, 2, tiled=True)


def solution(mesh):
    in_specs = (
        P(("groups", "band"), None, None, None),
        P("groups"),
        P(("groups", "band"), None),
        P(("groups", "band"), None),
        P(("groups", "band"), None),
        P(("groups", "band"), None, None),
    )
    out_specs = P(("groups", "band"), None, None, None)
    return jax.shard_map(shards, mesh=mesh, in_specs=in_specs, out_specs=out_specs, check_vma=False)
```

```python
import jax
import jax.numpy as jnp
from jax import lax
from jax.sharding import PartitionSpec as P
from jax.experimental import pallas as pl
from jax.experimental.pallas import tpu as pltpu

PREDICTION_COUNT = 4


exact = lax.Precision.HIGHEST
time_step = 0.25
viscous = 0.05
slow_friction = 0.2
control_weight = 0.5


def extended(shard, sides, width):
    for axis, dim in sides:
        devices, length = (lax.axis_size(axis), shard.shape[dim])
        up = [(i, (i + 1) % devices) for i in range(devices - 1)]
        down = [(j, i) for i, j in up]
        last = lax.slice_in_dim(shard, length - width, length, axis=dim)
        leading = lax.slice_in_dim(shard, 0, width, axis=dim)
        before = lax.ppermute(last, axis, up)
        after = lax.ppermute(leading, axis, down)
        shard = jnp.concatenate([before, shard, after], axis=dim)
    return shard


def neighbours(field):
    lon_pad = jnp.pad(field, [(0, 0)] * (field.ndim - 1) + [(1, 1)])
    lat_pad = jnp.pad(field, [(0, 0)] * (field.ndim - 2) + [(1, 1), (0, 0)])
    return (lon_pad[..., 2:], lon_pad[..., :-2], lat_pad[..., 2:, :], lat_pad[..., :-2, :])


def east_slope(field):
    ahead, behind, upper, lower = neighbours(field)
    return 0.5 * (ahead - behind)


def north_slope(field):
    ahead, behind, upper, lower = neighbours(field)
    return 0.5 * (upper - lower)


def laplace(field):
    ahead, behind, upper, lower = neighbours(field)
    return ahead + behind + upper + lower - 4.0 * field


def advance(height, eastward, northward, nonlinear, friction, coriolis):
    depth = 1.0 + nonlinear * height
    height_new = (
        height
        - time_step * (east_slope(depth * eastward) + north_slope(depth * northward))
        + time_step * viscous * laplace(height)
    )
    east_new = eastward + time_step * (
        -nonlinear * (eastward * east_slope(eastward) + northward * north_slope(eastward))
        + coriolis * northward
        - east_slope(height_new)
        + viscous * laplace(eastward)
        - friction * eastward
    )
    north_new = northward + time_step * (
        -nonlinear * (eastward * east_slope(northward) + northward * north_slope(northward))
        - coriolis * eastward
        - north_slope(height_new)
        + viscous * laplace(northward)
        - friction * northward
    )
    return (height_new, east_new, north_new)


def begin_prediction(marine_condition, accuracy_levels, realization_count):
    nonlinear = (accuracy_levels == 0).astype(jnp.float32)[:, None, None]
    friction = jnp.where(accuracy_levels == 0, 0.0, slow_friction).astype(jnp.float32)[
        :, None, None
    ]
    lat_rows = marine_condition.shape[2]
    coriolis = (0.1 + 0.2 * (jnp.arange(lat_rows).astype(jnp.float32) + 0.5) / lat_rows)[:, None]
    height, eastward, northward = (
        marine_condition[:, 0],
        marine_condition[:, 1],
        marine_condition[:, 2],
    )
    for step in range(realization_count):
        height, eastward, northward = advance(
            height, eastward, northward, nonlinear, friction, coriolis
        )
    return jnp.stack([height, eastward, northward], axis=1)


def class_tables(accuracy_levels):
    onehot = (accuracy_levels[:, None] == jnp.arange(3)[None, :]).astype(jnp.float32)
    counts = jnp.sum(onehot, axis=0)
    coefs = jnp.stack(
        [
            1.0 / (counts[0] - 1.0),
            -control_weight / (counts[1] - 1.0),
            control_weight / (counts[2] - 1.0),
        ]
    )
    member_weight = jnp.sum(onehot * coefs[None, :], axis=1)
    return (onehot, counts, member_weight)


def remove_means(data, onehot, counts):
    means = jnp.dot(onehot.T, data, precision=exact) / counts[:, None]
    return data - jnp.dot(onehot, means, precision=exact)


def spd_solve(factor, rhs):
    inner = lax.linalg.triangular_solve(factor, rhs, left_side=True, lower=True)
    return lax.linalg.triangular_solve(factor, inner, left_side=True, lower=True, transpose_a=True)


def gauss_jordan_steps(a):
    n = a.shape[0]
    lane = lax.broadcasted_iota(jnp.int32, a.shape, 1)
    row_id = lax.broadcasted_iota(jnp.int32, (n, 1), 0)
    if n <= 64:
        for k in range(n):
            pivot_row = a[k : k + 1, :] * (1.0 / a[k : k + 1, k : k + 1])
            column = a[:, k : k + 1] - (row_id == k).astype(jnp.float32)
            a = a - column * pivot_row
        return a

    def step(k, a):
        pivot_row = jnp.sum(jnp.where(row_id == k, a, 0.0), axis=0, keepdims=True)
        column = jnp.sum(jnp.where(lane == k, a, 0.0), axis=1, keepdims=True)
        pivot = jnp.sum(jnp.where(lane[0:1] == k, pivot_row, 0.0), axis=1, keepdims=True)
        pivot_row = pivot_row / pivot
        column = column - (row_id == k).astype(jnp.float32)
        return a - column * pivot_row

    return lax.fori_loop(0, n, step, a)

def contract(a, b, dims):
    return lax.dot_general(
        a, b, (dims, ((), ())), precision=exact, preferred_element_type=jnp.float32
    )


def analysis_kernel(
    cell_ref, below_ref, x_ref, above_ref, fid_col_ref, fid_row_ref, value_ref, var_ref, noise_ref,
    o_ref, cells_ref, picked_ref,
):
    per_device = fid_col_ref.shape[1]
    width = x_ref.shape[2] // per_device
    def members_of(ref):
        return jnp.concatenate([ref[:, 0, i * width : (i + 1) * width] for i in range(per_device)], axis=0)
    x = members_of(x_ref)
    m = x.shape[0]
    components = 3
    lon = width // components
    for offset, ref in enumerate((below_ref, x_ref, above_ref)):
        block = x if offset == 1 else members_of(ref)
        block = block.T
        for component in range(components):
            cells_ref[pl.ds((component * 3 + offset) * lon, lon), :] = block[component * lon : (component + 1) * lon]

    def pick(o, carry):
        picked_ref[pl.ds(o, 1), :] = cells_ref[pl.ds(cell_ref[o], 1), :]
        return carry

    lax.fori_loop(0, picked_ref.shape[0], pick, 0, unroll=picked_ref.shape[0] <= 512 or 8)
    ob = picked_ref[...].T
    fid_col = jnp.concatenate([fid_col_ref[:, i : i + 1] for i in range(per_device)], axis=0)
    fid_row = jnp.concatenate([fid_row_ref[i : i + 1, :] for i in range(per_device)], axis=1)
    variance = var_ref[...]
    masks = [(fid_col == c).astype(jnp.float32) for c in range(3)]
    masks_row = [(fid_row == c).astype(jnp.float32) for c in range(3)]
    counts = [jnp.sum(mask, axis=0, keepdims=True) for mask in masks]

    def remove_means(data):
        centred = data
        for mask, count in zip(masks, counts):
            centred = centred - mask * (jnp.sum(mask * data, axis=0, keepdims=True) / count)
        return centred

    spread = remove_means(x)
    obs_spread = remove_means(ob)
    weight = (
        masks[0] * (1.0 / (counts[0] - 1.0))
        + masks[1] * (-control_weight / (counts[1] - 1.0))
        + masks[2] * (control_weight / (counts[2] - 1.0))
    )
    scale_col = jnp.sqrt(masks[0] / (counts[0] - 1.0))
    count_row = jnp.sum(masks_row[0], axis=1, keepdims=True)
    scale_row = jnp.sqrt(masks_row[0] / (count_row - 1.0))
    weighted = obs_spread / variance
    inner = contract(weighted, obs_spread, ((1,), (1,)))
    direct = contract(weighted, noise_ref[...], ((1,), (0,))) - contract(weighted, ob, ((1,), (1,)))
    row_id = lax.broadcasted_iota(jnp.int32, (m, m), 0)
    col_id = lax.broadcasted_iota(jnp.int32, (m, m), 1)
    system = (row_id == col_id).astype(jnp.float32) + scale_col * inner * scale_row
    augmented = jnp.concatenate([system, scale_col * direct], axis=1)
    solved = gauss_jordan_steps(augmented)[:, m:]
    projected = direct - contract(inner, scale_col * solved, ((1,), (0,)))
    mixing = projected * weight
    result = x + contract(mixing, spread, ((0,), (0,)))
    sources = x_ref.shape[0]
    for i in range(per_device):
        for component in range(components):
            o_ref[i, component] = result[i * sources : (i + 1) * sources, component * lon : (component + 1) * lon]


def analysis(cells, below, rows, above, fidelity, value, variance, noise):
    sources = rows.shape[0]
    members = fidelity.shape[0]
    vmem = pl.BlockSpec(memory_space=pltpu.VMEM)
    return pl.pallas_call(
        analysis_kernel,
        out_shape=jax.ShapeDtypeStruct((members // sources, 3, sources, rows.shape[2] // (3 * members // sources)), jnp.float32),
        in_specs=[pl.BlockSpec(memory_space=pltpu.SMEM)] + [vmem] * 8,
        out_specs=vmem,
        scratch_shapes=[
            pltpu.VMEM((3 * rows.shape[2] // (members // sources), members), jnp.float32),
            pltpu.VMEM((cells.shape[0], members), jnp.float32),
        ],
        compiler_params=pltpu.CompilerParams(vmem_limit_bytes=48 * 1024 * 1024),
    )(
        cells,
        below,
        rows,
        above,
        fidelity.reshape(sources, -1),
        fidelity.reshape(sources, -1).T,
        value.reshape(1, -1),
        variance.reshape(1, -1),
        noise,
    )


def shifted(field, offset, axis):
    size = field.shape[axis]
    rolled = pltpu.roll(field, (-offset) % size, axis)
    place = lax.broadcasted_iota(jnp.int32, field.shape, axis) + offset
    return jnp.where((place >= 0) & (place < size), rolled, 0.0)


def kernel_neighbours(field):
    return (shifted(field, 1, 1), shifted(field, -1, 1), shifted(field, 1, 0), shifted(field, -1, 0))


def kernel_east(field):
    ahead, behind, upper, lower = kernel_neighbours(field)
    return 0.5 * (ahead - behind)


def kernel_north(field):
    ahead, behind, upper, lower = kernel_neighbours(field)
    return 0.5 * (upper - lower)


def kernel_laplace(field):
    ahead, behind, upper, lower = kernel_neighbours(field)
    return ahead + behind + upper + lower - 4.0 * field


def forecast_kernel(fid_ref, x_ref, o_ref):
    members, _, lat_rows, lon = x_ref.shape
    first = lax.axis_index("band") * members
    row = lax.broadcasted_iota(jnp.int32, (lat_rows, 1), 0).astype(jnp.float32)
    coriolis = 0.1 + 0.2 * (row + 0.5) / lat_rows
    for member in range(members):
        level = fid_ref[first + member]
        nonlinear = jnp.where(level == 0, 1.0, 0.0).astype(jnp.float32)
        friction = jnp.where(level == 0, 0.0, slow_friction).astype(jnp.float32)
        height, eastward, northward = x_ref[member, 0], x_ref[member, 1], x_ref[member, 2]
        keep = 1.0 - time_step * friction
        advect = -nonlinear * (0.5 * time_step)
        turn = time_step * coriolis
        for step in range(PREDICTION_COUNT):
            depth = 1.0 + nonlinear * height
            east_flux, north_flux = depth * eastward, depth * northward
            h_ahead, h_behind, h_upper, h_lower = kernel_neighbours(height)
            height_new = (
                height
                - (0.5 * time_step)
                * ((shifted(east_flux, 1, 1) - shifted(east_flux, -1, 1)) + (shifted(north_flux, 1, 0) - shifted(north_flux, -1, 0)))
                + (time_step * viscous) * ((h_ahead + h_behind) + (h_upper + h_lower) - 4.0 * height)
            )
            n_ahead, n_behind, n_upper, n_lower = kernel_neighbours(height_new)
            u_ahead, u_behind, u_upper, u_lower = kernel_neighbours(eastward)
            v_ahead, v_behind, v_upper, v_lower = kernel_neighbours(northward)
            east_new = (
                keep * eastward
                + advect * (eastward * (u_ahead - u_behind) + northward * (u_upper - u_lower))
                + turn * northward
                - (0.5 * time_step) * (n_ahead - n_behind)
                + (time_step * viscous) * ((u_ahead + u_behind) + (u_upper + u_lower) - 4.0 * eastward)
            )
            north_new = (
                keep * northward
                + advect * (eastward * (v_ahead - v_behind) + northward * (v_upper - v_lower))
                - turn * eastward
                - (0.5 * time_step) * (n_upper - n_lower)
                + (time_step * viscous) * ((v_ahead + v_behind) + (v_upper + v_lower) - 4.0 * northward)
            )
            height, eastward, northward = height_new, east_new, north_new
        for component, field in enumerate((height, eastward, northward)):
            o_ref[:, 0, pl.ds((member * 3 + component) * lon, lon)] = field


def forecast(initial, levels):
    members, components, lat_rows, lon = initial.shape
    return pl.pallas_call(
        forecast_kernel,
        out_shape=jax.ShapeDtypeStruct((lat_rows, 1, members * components * lon), jnp.float32),
        in_specs=[
            pl.BlockSpec(memory_space=pltpu.SMEM),
            pl.BlockSpec(memory_space=pltpu.VMEM),
        ],
        out_specs=pl.BlockSpec(memory_space=pltpu.VMEM),
    )(levels, initial)


def shards(initial_height_velocity, member_fidelity, obs_cell, obs_value, obs_var, obs_noise):
    per_device, components, lat_rows, lon = initial_height_velocity.shape
    sources = lax.axis_size("band")
    rows = forecast(initial_height_velocity, member_fidelity)
    rows = lax.all_to_all(rows, "band", 0, 0, tiled=True)
    up = [(i, i + 1) for i in range(sources - 1)]
    down = [(j, i) for i, j in up]
    below = lax.ppermute(rows, "band", up)
    above = lax.ppermute(rows, "band", down)
    noise = obs_noise[0].reshape(-1, sources, per_device)
    noise = jnp.transpose(noise, (0, 2, 1)).reshape(-1, sources * per_device)
    noise = obs_value[0][:, None] + jnp.sqrt(obs_var[0])[:, None] * noise
    cells = jnp.clip(obs_cell[0], 0, 9 * lon - 1)
    result = analysis(cells, below, rows, above, member_fidelity, obs_value[0] + 0.0 * obs_var[0], obs_var[0], noise)
    return lax.all_to_all(result, "band", 2, 2, tiled=True)


def solution(mesh):
    in_specs = (
        P(("groups", "band"), None, None, None),
        P("groups"),
        P(("groups", "band"), None),
        P(("groups", "band"), None),
        P(("groups", "band"), None),
        P(("groups", "band"), None, None),
    )
    out_specs = P(("groups", "band"), None, None, None)
    return jax.shard_map(shards, mesh=mesh, in_specs=in_specs, out_specs=out_specs, check_vma=False)
```
